768 devices in a mesh: grp: 4 (over z_hi, core), lon: 48 (over z_lo, y), lat: 4 (over x).
Axes of the slice: x: 4, y: 8, z: 12 (z_hi: 2, z_lo: 6; z = z_hi * 6 + z_lo), core: 2. Of those that a mesh axis runs over, the one named last changes fastest.
Arguments:
- state: float32 [4, 40, 1152, 512], P('grp', None, 'lon', 'lat'), may hold values from -6 to 6
- depth: int32 [1152, 512], P('lon', 'lat'), may hold values from 0 to 6
- rates: float32 [20, 20], replicated, may hold values from -1.25 to 1.25
- grazing: float32 [20], replicated, may hold values from -3 to 3
Outputs:
- state_out: float32 [4, 40, 1152, 512], P('grp', None, 'lon', 'lat')
The draws below stay inside these ranges and needn't reach their ends.
Inputs may be any that keep to these rules, and one draw needn't show every extreme that they name: `depth`: number of wet levels of a column; 0 is land.
All inputs are finite; a program needn't handle non-finite values.
Results may differ from the reference program's by a relative error of at most 0.0003.
Values sent between devices are 32-bit elements; how exact they have to be, the bound alone decides.
No kernel may reach another device: no remote copies, remote signals or barrier semaphores. Data moves between devices by JAX's collectives and lax.ppermute only.
A program may use at most 32 MiB of HBM per device.

```python
import jax
import jax.numpy as jnp
from jax import lax

LZ = 2
NTR = 20
SECTIONS = 4
NSUB = 4
NZ = 6
NX = 1152
NY = 512
NF = 40
N_GRP = 4


def with_ends(array, stream_key, least, largest):
    longest = array.shape.index(max(array.shape))
    spots = []
    for shift in (0, 1):
        where = [jax.random.randint(jax.random.fold_in(stream_key, axis), (), 0, length) for axis, length in enumerate(array.shape)]
        where[longest] = (where[longest] + shift) % array.shape[longest]
        spots.append(tuple(where))
    return array.at[spots[0]].set(least).at[spots[1]].set(largest)


def levels(own_key, extent, shards, smallest, largest):
    level, own = 1.0, jax.random.fold_in(own_key, 6)
    for dim, parts in shards:
        heights = jnp.exp(jax.random.uniform(jax.random.fold_in(own, dim), (parts,), jnp.float32, smallest / len(shards), largest / len(shards)))
        level = level * jnp.repeat(heights, extent[dim] // parts).reshape([-1 if axis == dim else 1 for axis in range(len(extent))])
    return level


def noise(own_key, dims, width, bound, split=(), kind=jnp.bfloat16):
    level = levels(own_key, dims, split, -0.22, 0.18) if split else 1.0
    values = jax.random.normal(own_key, dims, jnp.float32) * width * level
    return jnp.minimum(jnp.maximum(values, -bound), bound).astype(kind)


def setup_inputs(seed: int = 0) -> dict:
    seeds = jax.random.split(jax.random.key(seed), 5)
    return {
        "state": noise(seeds[0], (N_GRP, NF, NX, NY), 1.0, 6.0, ((0, 4), (2, 48), (3, 4)), jnp.float32),
        "depth": with_ends(jax.random.randint(seeds[1], (NX, NY), 0, NZ + 1), jax.random.fold_in(seeds[1], 1), 0, NZ).astype(jnp.int32),
        "rates": noise(seeds[2], (NTR, NTR), NTR ** -0.5, 1.25, (), jnp.float32),
        "grazing": noise(seeds[3], (NTR,), 0.5, 3.0, (), jnp.float32),
    }


def pad_grid(field):
    field = jnp.concatenate([field[..., -1:, :], field, field[..., :1, :]], axis=-2)
    zeros_rim = jnp.zeros(field.shape[:-1] + (1,), field.dtype)
    return jnp.concatenate([zeros_rim, field, zeros_rim], axis=-1)


def center_of(padded):
    return padded[..., 1:-1, 1:-1]


def grad_x(padded):
    return padded[..., 2:, 1:-1] - padded[..., :-2, 1:-1]


def grad_y(padded):
    return padded[..., 1:-1, 2:] - padded[..., 1:-1, :-2]


def laplace(padded):
    return padded[..., 2:, 1:-1] + padded[..., :-2, 1:-1] + padded[..., 1:-1, 2:] + padded[..., 1:-1, :-2] - 4.0 * center_of(padded)


def advance_dynamics(zonal_pad, merid_pad, temp_pad, surf_pad, wet_mask, land_mask, coriolis_rows):
    zonal = center_of(zonal_pad)
    merid = center_of(merid_pad)
    temper = center_of(temp_pad)
    surface = center_of(surf_pad)
    divergence = jnp.sum(grad_x(zonal_pad) + grad_y(merid_pad), axis=0)
    zonal_new = wet_mask * (zonal + coriolis_rows * merid - 0.5 * grad_x(surf_pad))
    merid_new = wet_mask * (merid - coriolis_rows * zonal - 0.5 * grad_y(surf_pad))
    surface_new = land_mask * (surface - (0.25 / zonal.shape[0]) * divergence)
    temper_new = wet_mask * (temper - 0.25 * (zonal * grad_x(temp_pad) + merid * grad_y(temp_pad)) + 0.1 * laplace(temp_pad))
    return zonal_new, merid_new, temper_new, surface_new


def advect_tracers(tracer_pad, zonal, merid, wet_mask):
    return wet_mask * (center_of(tracer_pad) - 0.25 * (zonal * grad_x(tracer_pad) + merid * grad_y(tracer_pad)) + 0.1 * laplace(tracer_pad))


def reference(state, depth, rates, grazing):
    groups = N_GRP
    level_index = jnp.arange(NZ, dtype=jnp.int32)[:, None, None]
    wet_mask = (level_index < depth[None]).astype(state.dtype)
    land_mask = (depth > 0).astype(state.dtype)
    lat_coord = jnp.arange(NY).astype(state.dtype)
    coriolis_rows = 0.3 * jnp.sin(jnp.pi * (lat_coord + 0.5) / NY - jnp.pi / 2)
    dynamic = state[0]
    zonal = dynamic[:NZ]
    merid = dynamic[NZ:2 * NZ]
    temper = dynamic[2 * NZ:3 * NZ]
    surface = dynamic[3 * NZ]
    for section_index in range(SECTIONS):
        zonal, merid, temper, surface = advance_dynamics(pad_grid(zonal), pad_grid(merid), pad_grid(temper), pad_grid(surface), wet_mask, land_mask, coriolis_rows)
    tracers = state[1:].reshape(groups - 1, NTR, LZ, NX, NY)
    tracers = jnp.transpose(tracers, (1, 0, 2, 3, 4)).reshape(NTR, NZ, NX, NY)

    def transport(single):
        for sub_index in range(NSUB):
            single = advect_tracers(pad_grid(single), zonal, merid, wet_mask)
        return single

    tracers = lax.map(transport, tracers)
    kinetic = jnp.einsum('ts,szxy->tzxy', rates, tracers, precision=lax.Precision.HIGHEST)
    kinetic = kinetic + grazing[:, None, None, None] * (tracers[0] * tracers[1])[None]
    updated = wet_mask[None] * (tracers + 0.2 * jnp.exp(0.05 * temper)[None] * kinetic)
    light_factor = jnp.exp(-(level_index.astype(state.dtype) + 0.5) / NZ)
    heating = 0.3 * wet_mask * updated[0] * light_factor
    temper_final = temper + heating
    unused = jnp.zeros((NF - 3 * NZ - 1, NX, NY), state.dtype)
    first_slot = jnp.concatenate([zonal, merid, temper_final, surface[None], unused], axis=0)
    tracer_slots = updated.reshape(NTR, groups - 1, LZ, NX, NY)
    tracer_slots = jnp.transpose(tracer_slots, (1, 0, 2, 3, 4)).reshape(groups - 1, NF, NX, NY)
    return jnp.concatenate([first_slot[None], tracer_slots], axis=0)
```

```python
import jax
import jax.numpy as jnp
from jax import lax
from jax.sharding import PartitionSpec as P

LZ = 2
NTR = 20
SECTIONS = 4
NSUB = 4


def exchange(block, width, lat_pos, lat_count):
    for axis, dim in (("lon", 1), ("lat", 2)):
        count = lax.axis_size(axis)
        forward = [(i, (i + 1) % count) for i in range(count)]
        backward = [(target, source) for source, target in forward]
        low = lax.ppermute(
            lax.slice_in_dim(block, block.shape[dim] - width, None, axis=dim), axis, forward
        )
        high = lax.ppermute(lax.slice_in_dim(block, 0, width, axis=dim), axis, backward)
        block = jnp.concatenate([low, block, high], axis=dim)
    length = block.shape[-1]
    positions = jnp.arange(length)
    lower = (positions < width) & (lat_pos == 0)
    upper = (positions >= length - width) & (lat_pos == lat_count - 1)
    return jnp.where(lower | upper, 0.0, block)


def crop(array, from_radius, to_radius):
    cut = from_radius - to_radius
    if cut == 0:
        return array
    return array[..., cut : array.shape[-2] - cut, cut : array.shape[-1] - cut]


def center_of(padded):
    return padded[..., 1:-1, 1:-1]


def grad_x(padded):
    return padded[..., 2:, 1:-1] - padded[..., :-2, 1:-1]


def grad_y(padded):
    return padded[..., 1:-1, 2:] - padded[..., 1:-1, :-2]


def laplace(padded):
    return (
        padded[..., 2:, 1:-1]
        + padded[..., :-2, 1:-1]
        + padded[..., 1:-1, 2:]
        + padded[..., 1:-1, :-2]
        - 4.0 * center_of(padded)
    )


def advance_dynamics(zonal_pad, merid_pad, temp_pad, surf_pad, wet_mask, land_mask, coriolis_rows):
    zonal = center_of(zonal_pad)
    merid = center_of(merid_pad)
    temper = center_of(temp_pad)
    surface = center_of(surf_pad)
    divergence = jnp.sum(grad_x(zonal_pad) + grad_y(merid_pad), axis=0)
    zonal_new = wet_mask * (zonal + coriolis_rows * merid - 0.5 * grad_x(surf_pad))
    merid_new = wet_mask * (merid - coriolis_rows * zonal - 0.5 * grad_y(surf_pad))
    surface_new = land_mask * (surface - 0.25 / zonal.shape[0] * divergence)
    temper_new = wet_mask * (
        temper
        - 0.25 * (zonal * grad_x(temp_pad) + merid * grad_y(temp_pad))
        + 0.1 * laplace(temp_pad)
    )
    return (zonal_new, merid_new, temper_new, surface_new)


def advect_tracers(tracer_pad, zonal, merid, wet_mask):
    return wet_mask * (
        center_of(tracer_pad)
        - 0.25 * (zonal * grad_x(tracer_pad) + merid * grad_y(tracer_pad))
        + 0.1 * laplace(tracer_pad)
    )


def section_rows(padded, wet_mask, land_mask, coriolis_rows):
    levels = (padded.shape[0] - 1) // 3
    results = advance_dynamics(
        padded[:levels],
        padded[levels : 2 * levels],
        padded[2 * levels : 3 * levels],
        padded[3 * levels],
        wet_mask,
        land_mask,
        coriolis_rows,
    )
    return jnp.concatenate([results[0], results[1], results[2], results[3][None]], axis=0)


def body(state, depth, rates, grazing):
    groups = lax.axis_size("grp")
    member = lax.axis_index("grp")
    lat_pos = lax.axis_index("lat")
    lat_count = lax.axis_size("lat")
    local = state[0]
    field_rows, columns, lat_rows = local.shape
    total_levels = LZ * (groups - 1)
    dyn_rows = 3 * total_levels + 1
    lat_total = lat_rows * lat_count
    dyn_halo = SECTIONS + NSUB - 1
    tracer_halo = NSUB
    vel_halo = NSUB - 1

    depth_f = depth.astype(jnp.float32)
    block = jnp.concatenate([local, depth_f[None]], axis=0)
    padded = exchange(block, dyn_halo, lat_pos, lat_count)
    depth_pad = padded[field_rows]

    level_index = jnp.arange(total_levels).astype(jnp.float32)[:, None, None]
    wet_pad = (level_index < depth_pad[None]).astype(jnp.float32)
    land_pad = (depth_pad > 0).astype(jnp.float32)
    coord = (lat_pos * lat_rows - dyn_halo + jnp.arange(lat_rows + 2 * dyn_halo)).astype(jnp.float32)
    coriolis_pad = 0.3 * jnp.sin(jnp.pi * (coord + 0.5) / lat_total - jnp.pi / 2)

    current = padded[:dyn_rows]
    radius = dyn_halo
    for section_index in range(SECTIONS):
        radius -= 1
        cut = dyn_halo - radius
        current = section_rows(
            current,
            crop(wet_pad, dyn_halo, radius),
            crop(land_pad, dyn_halo, radius),
            coriolis_pad[cut : coriolis_pad.shape[0] - cut],
        )
    zonal_r = current[:total_levels]
    merid_r = current[total_levels : 2 * total_levels]
    temper_r = current[2 * total_levels : 3 * total_levels]
    zonal = crop(zonal_r, radius, 0)
    merid = crop(merid_r, radius, 0)
    temper = crop(temper_r, radius, 0)
    surface = crop(current[3 * total_levels], radius, 0)

    first_level = jnp.maximum(member - 1, 0) * LZ
    vcols, vrows = zonal_r.shape[-2:]
    forcing = jnp.stack(
        [
            zonal_r.reshape(groups - 1, LZ, vcols, vrows),
            merid_r.reshape(groups - 1, LZ, vcols, vrows),
            temper_r.reshape(groups - 1, LZ, vcols, vrows),
        ],
        axis=1,
    )
    outgoing = jnp.concatenate([jnp.zeros((1,) + forcing.shape[1:], jnp.float32), forcing], axis=0)
    received = lax.all_to_all(outgoing, "grp", split_axis=0, concat_axis=0, tiled=True)
    own_zonal = received[0, 0]
    own_merid = received[0, 1]
    own_temper = crop(received[0, 2], vel_halo, 0)

    member_levels = (first_level + jnp.arange(LZ)).astype(jnp.float32)[:, None, None]
    wet_member_pad = (member_levels < depth_pad[None]).astype(jnp.float32)
    tracers = crop(padded[:field_rows], dyn_halo, tracer_halo)
    advected = tracers.reshape((NTR, LZ) + tracers.shape[1:])
    radius = tracer_halo
    for sub_index in range(NSUB):
        radius -= 1
        advected = advect_tracers(
            advected,
            crop(own_zonal, vel_halo, radius),
            crop(own_merid, vel_halo, radius),
            crop(wet_member_pad, dyn_halo, radius),
        )
    wet_member = crop(wet_member_pad, dyn_halo, 0)
    kinetic = jnp.einsum("ts,szxy->tzxy", rates, advected, precision=lax.Precision.HIGHEST)
    kinetic = kinetic + grazing[:, None, None, None] * (advected[0] * advected[1])[None]
    updated = wet_member[None] * (advected + 0.2 * jnp.exp(0.05 * own_temper)[None] * kinetic)
    light_factor = jnp.exp(-(member_levels + 0.5) / total_levels)
    heating = 0.3 * wet_member * updated[0] * light_factor
    heat_out = jnp.concatenate(
        [heating[None], jnp.zeros((groups - 1,) + heating.shape, jnp.float32)], axis=0
    )
    returned = lax.all_to_all(heat_out, "grp", split_axis=0, concat_axis=0, tiled=True)
    temper_final = temper + returned[1:].reshape(total_levels, columns, lat_rows)
    unused = jnp.zeros((field_rows - dyn_rows, columns, lat_rows), jnp.float32)
    dyn_out = jnp.concatenate([zonal, merid, temper_final, surface[None], unused], axis=0)
    result = jnp.where(member == 0, dyn_out, updated.reshape(field_rows, columns, lat_rows))
    return result[None]


def solution(mesh):
    in_specs = (P("grp", None, "lon", "lat"), P("lon", "lat"), P(), P())
    out_specs = P("grp", None, "lon", "lat")
    return jax.shard_map(body, mesh=mesh, in_specs=in_specs, out_specs=out_specs, check_vma=False)
```

```python
import jax
import jax.numpy as jnp
from jax import lax
from jax.sharding import PartitionSpec as P

LZ = 2
NTR = 20
SECTIONS = 4
NSUB = 4


def exchange(block, width, lat_pos, lat_count):
    for axis, dim in (("lon", 1), ("lat", 2)):
        count = lax.axis_size(axis)
        forward = [(i, (i + 1) % count) for i in range(count)]
        backward = [(target, source) for source, target in forward]
        low = lax.ppermute(
            lax.slice_in_dim(block, block.shape[dim] - width, None, axis=dim), axis, forward
        )
        high = lax.ppermute(lax.slice_in_dim(block, 0, width, axis=dim), axis, backward)
        block = jnp.concatenate([low, block, high], axis=dim)
    length = block.shape[-1]
    positions = jnp.arange(length)
    lower = (positions < width) & (lat_pos == 0)
    upper = (positions >= length - width) & (lat_pos == lat_count - 1)
    return jnp.where(lower | upper, 0.0, block)


def crop(array, from_radius, to_radius):
    cut = from_radius - to_radius
    if cut == 0:
        return array
    return array[..., cut : array.shape[-2] - cut, cut : array.shape[-1] - cut]


def center_of(padded):
    return padded[..., 1:-1, 1:-1]


def grad_x(padded):
    return padded[..., 2:, 1:-1] - padded[..., :-2, 1:-1]


def grad_y(padded):
    return padded[..., 1:-1, 2:] - padded[..., 1:-1, :-2]


def laplace(padded):
    return (
        padded[..., 2:, 1:-1]
        + padded[..., :-2, 1:-1]
        + padded[..., 1:-1, 2:]
        + padded[..., 1:-1, :-2]
        - 4.0 * center_of(padded)
    )


def advance_dynamics(zonal_pad, merid_pad, temp_pad, surf_pad, wet_mask, land_mask, coriolis_rows):
    zonal = center_of(zonal_pad)
    merid = center_of(merid_pad)
    temper = center_of(temp_pad)
    surface = center_of(surf_pad)
    divergence = jnp.sum(grad_x(zonal_pad) + grad_y(merid_pad), axis=0)
    zonal_new = wet_mask * (zonal + coriolis_rows * merid - 0.5 * grad_x(surf_pad))
    merid_new = wet_mask * (merid - coriolis_rows * zonal - 0.5 * grad_y(surf_pad))
    surface_new = land_mask * (surface - 0.25 / zonal.shape[0] * divergence)
    temper_new = wet_mask * (
        temper
        - 0.25 * (zonal * grad_x(temp_pad) + merid * grad_y(temp_pad))
        + 0.1 * laplace(temp_pad)
    )
    return (zonal_new, merid_new, temper_new, surface_new)


def advect_tracers(tracer_pad, zonal, merid, wet_mask):
    return wet_mask * (
        center_of(tracer_pad)
        - 0.25 * (zonal * grad_x(tracer_pad) + merid * grad_y(tracer_pad))
        + 0.1 * laplace(tracer_pad)
    )


def section_rows(padded, wet_mask, land_mask, coriolis_rows):
    levels = (padded.shape[0] - 1) // 3
    results = advance_dynamics(
        padded[:levels],
        padded[levels : 2 * levels],
        padded[2 * levels : 3 * levels],
        padded[3 * levels],
        wet_mask,
        land_mask,
        coriolis_rows,
    )
    return jnp.concatenate([results[0], results[1], results[2], results[3][None]], axis=0)


def body(state, depth, rates, grazing):
    groups = lax.axis_size("grp")
    member = lax.axis_index("grp")
    lat_pos = lax.axis_index("lat")
    lat_count = lax.axis_size("lat")
    local = state[0]
    field_rows, columns, lat_rows = local.shape
    total_levels = LZ * (groups - 1)
    dyn_rows = 3 * total_levels + 1
    lat_total = lat_rows * lat_count
    dyn_halo = SECTIONS + NSUB - 1
    tracer_halo = NSUB
    vel_halo = NSUB - 1

    depth_f = depth.astype(jnp.float32)
    block = jnp.concatenate([local, depth_f[None]], axis=0)
    padded = exchange(block, dyn_halo, lat_pos, lat_count)
    depth_pad = padded[field_rows]

    level_index = jnp.arange(total_levels).astype(jnp.float32)[:, None, None]
    wet_pad = (level_index < depth_pad[None]).astype(jnp.float32)
    land_pad = (depth_pad > 0).astype(jnp.float32)
    coord = (lat_pos * lat_rows - dyn_halo + jnp.arange(lat_rows + 2 * dyn_halo)).astype(jnp.float32)
    coriolis_pad = 0.3 * jnp.sin(jnp.pi * (coord + 0.5) / lat_total - jnp.pi / 2)

    current = padded[:dyn_rows]
    radius = dyn_halo
    for section_index in range(SECTIONS):
        radius -= 1
        cut = dyn_halo - radius
        current = section_rows(
            current,
            crop(wet_pad, dyn_halo, radius),
            crop(land_pad, dyn_halo, radius),
            coriolis_pad[cut : coriolis_pad.shape[0] - cut],
        )
    zonal_r = current[:total_levels]
    merid_r = current[total_levels : 2 * total_levels]
    temper_r = current[2 * total_levels : 3 * total_levels]
    zonal = crop(zonal_r, radius, 0)
    merid = crop(merid_r, radius, 0)
    temper = crop(temper_r, radius, 0)
    surface = crop(current[3 * total_levels], radius, 0)

    first_level = jnp.maximum(member - 1, 0) * LZ
    vcols, vrows = zonal_r.shape[-2:]
    forcing = jnp.stack(
        [
            zonal_r.reshape(groups - 1, LZ, vcols, vrows),
            merid_r.reshape(groups - 1, LZ, vcols, vrows),
            temper_r.reshape(groups - 1, LZ, vcols, vrows),
        ],
        axis=1,
    )
    own = forcing[0]
    for shift in range(1, groups):
        pairs = [(i, (i + shift) % groups) for i in range(groups)]
        arrived = lax.ppermute(forcing[shift - 1], "grp", pairs)
        own = jnp.where(member == shift, arrived, own)
    own_zonal = own[0]
    own_merid = own[1]
    own_temper = crop(own[2], vel_halo, 0)

    member_levels = (first_level + jnp.arange(LZ)).astype(jnp.float32)[:, None, None]
    wet_member_pad = (member_levels < depth_pad[None]).astype(jnp.float32)
    tracers = crop(padded[:field_rows], dyn_halo, tracer_halo)
    advected = tracers.reshape((NTR, LZ) + tracers.shape[1:])
    radius = tracer_halo
    for sub_index in range(NSUB):
        radius -= 1
        advected = advect_tracers(
            advected,
            crop(own_zonal, vel_halo, radius),
            crop(own_merid, vel_halo, radius),
            crop(wet_member_pad, dyn_halo, radius),
        )
    wet_member = crop(wet_member_pad, dyn_halo, 0)
    kinetic = jnp.einsum("ts,szxy->tzxy", rates, advected, precision=lax.Precision.HIGHEST)
    kinetic = kinetic + grazing[:, None, None, None] * (advected[0] * advected[1])[None]
    updated = wet_member[None] * (advected + 0.2 * jnp.exp(0.05 * own_temper)[None] * kinetic)
    light_factor = jnp.exp(-(member_levels + 0.5) / total_levels)
    heating = 0.3 * wet_member * updated[0] * light_factor
    returned = []
    for shift in range(1, groups):
        pairs = [(i, (i - shift) % groups) for i in range(groups)]
        returned.append(lax.ppermute(heating, "grp", pairs))
    returned = jnp.concatenate(returned, axis=0)
    temper_final = temper + returned
    unused = jnp.zeros((field_rows - dyn_rows, columns, lat_rows), jnp.float32)
    dyn_out = jnp.concatenate([zonal, merid, temper_final, surface[None], unused], axis=0)
    result = jnp.where(member == 0, dyn_out, updated.reshape(field_rows, columns, lat_rows))
    return result[None]


def solution(mesh):
    in_specs = (P("grp", None, "lon", "lat"), P("lon", "lat"), P(), P())
    out_specs = P("grp", None, "lon", "lat")
    return jax.shard_map(body, mesh=mesh, in_specs=in_specs, out_specs=out_specs, check_vma=False)
```

```python
import jax
import jax.numpy as jnp
from jax import lax
from jax.sharding import PartitionSpec as P

LZ = 2
NTR = 20
SECTIONS = 4
NSUB = 4


def exchange(block, width, lat_pos, lat_count):
    for axis, dim in (("lon", 1), ("lat", 2)):
        count = lax.axis_size(axis)
        forward = [(i, (i + 1) % count) for i in range(count)]
        backward = [(target, source) for source, target in forward]
        low = lax.ppermute(
            lax.slice_in_dim(block, block.shape[dim] - width, None, axis=dim), axis, forward
        )
        high = lax.ppermute(lax.slice_in_dim(block, 0, width, axis=dim), axis, backward)
        block = jnp.concatenate([low, block, high], axis=dim)
    length = block.shape[-1]
    positions = jnp.arange(length)
    lower = (positions < width) & (lat_pos == 0)
    upper = (positions >= length - width) & (lat_pos == lat_count - 1)
    return jnp.where(lower | upper, 0.0, block)


def crop(array, from_radius, to_radius):
    cut = from_radius - to_radius
    if cut == 0:
        return array
    return array[..., cut : array.shape[-2] - cut, cut : array.shape[-1] - cut]


def center_of(padded):
    return padded[..., 1:-1, 1:-1]


def grad_x(padded):
    return padded[..., 2:, 1:-1] - padded[..., :-2, 1:-1]


def grad_y(padded):
    return padded[..., 1:-1, 2:] - padded[..., 1:-1, :-2]


def laplace(padded):
    return (
        padded[..., 2:, 1:-1]
        + padded[..., :-2, 1:-1]
        + padded[..., 1:-1, 2:]
        + padded[..., 1:-1, :-2]
        - 4.0 * center_of(padded)
    )


def advance_dynamics(zonal_pad, merid_pad, temp_pad, surf_pad, wet_mask, land_mask, coriolis_rows):
    zonal = center_of(zonal_pad)
    merid = center_of(merid_pad)
    temper = center_of(temp_pad)
    surface = center_of(surf_pad)
    divergence = jnp.sum(grad_x(zonal_pad) + grad_y(merid_pad), axis=0)
    zonal_new = wet_mask * (zonal + coriolis_rows * merid - 0.5 * grad_x(surf_pad))
    merid_new = wet_mask * (merid - coriolis_rows * zonal - 0.5 * grad_y(surf_pad))
    surface_new = land_mask * (surface - 0.25 / zonal.shape[0] * divergence)
    temper_new = wet_mask * (
        temper
        - 0.25 * (zonal * grad_x(temp_pad) + merid * grad_y(temp_pad))
        + 0.1 * laplace(temp_pad)
    )
    return (zonal_new, merid_new, temper_new, surface_new)


def advect_tracers(tracer_pad, zonal, merid, wet_mask):
    return wet_mask * (
        center_of(tracer_pad)
        - 0.25 * (zonal * grad_x(tracer_pad) + merid * grad_y(tracer_pad))
        + 0.1 * laplace(tracer_pad)
    )


def section_rows(padded, wet_mask, land_mask, coriolis_rows):
    levels = (padded.shape[0] - 1) // 3
    results = advance_dynamics(
        padded[:levels],
        padded[levels : 2 * levels],
        padded[2 * levels : 3 * levels],
        padded[3 * levels],
        wet_mask,
        land_mask,
        coriolis_rows,
    )
    return jnp.concatenate([results[0], results[1], results[2], results[3][None]], axis=0)


def body(state, depth, rates, grazing):
    groups = lax.axis_size("grp")
    member = lax.axis_index("grp")
    lat_pos = lax.axis_index("lat")
    lat_count = lax.axis_size("lat")
    local = state[0]
    field_rows, columns, lat_rows = local.shape
    total_levels = LZ * (groups - 1)
    dyn_rows = 3 * total_levels + 1
    lat_total = lat_rows * lat_count
    dyn_halo = SECTIONS + NSUB - 1
    tracer_halo = NSUB
    vel_halo = NSUB - 1

    depth_f = depth.astype(jnp.float32)
    block = jnp.concatenate([local, depth_f[None]], axis=0)
    padded = exchange(block, dyn_halo, lat_pos, lat_count)
    depth_pad = padded[field_rows]

    level_index = jnp.arange(total_levels).astype(jnp.float32)[:, None, None]
    wet_pad = (level_index < depth_pad[None]).astype(jnp.float32)
    land_pad = (depth_pad > 0).astype(jnp.float32)
    coord = (lat_pos * lat_rows - dyn_halo + jnp.arange(lat_rows + 2 * dyn_halo)).astype(jnp.float32)
    coriolis_pad = 0.3 * jnp.sin(jnp.pi * (coord + 0.5) / lat_total - jnp.pi / 2)

    current = padded[:dyn_rows]
    radius = dyn_halo
    for section_index in range(SECTIONS):
        radius -= 1
        cut = dyn_halo - radius
        current = section_rows(
            current,
            crop(wet_pad, dyn_halo, radius),
            crop(land_pad, dyn_halo, radius),
            coriolis_pad[cut : coriolis_pad.shape[0] - cut],
        )
    zonal_r = current[:total_levels]
    merid_r = current[total_levels : 2 * total_levels]
    temper_r = current[2 * total_levels : 3 * total_levels]
    zonal = crop(zonal_r, radius, 0)
    merid = crop(merid_r, radius, 0)
    temper = crop(temper_r, radius, 0)
    surface = crop(current[3 * total_levels], radius, 0)

    first_level = jnp.maximum(member - 1, 0) * LZ
    vcols, vrows = zonal_r.shape[-2:]
    forcing = jnp.stack(
        [
            zonal_r.reshape(groups - 1, LZ, vcols, vrows),
            merid_r.reshape(groups - 1, LZ, vcols, vrows),
            temper_r.reshape(groups - 1, LZ, vcols, vrows),
        ],
        axis=1,
    )
    own = forcing[0]
    for shift in range(1, groups):
        pairs = [(0, shift)]
        arrived = lax.ppermute(forcing[shift - 1], "grp", pairs)
        own = jnp.where(member == shift, arrived, own)
    own_zonal = own[0]
    own_merid = own[1]
    own_temper = crop(own[2], vel_halo, 0)

    member_levels = (first_level + jnp.arange(LZ)).astype(jnp.float32)[:, None, None]
    wet_member_pad = (member_levels < depth_pad[None]).astype(jnp.float32)
    tracers = crop(padded[:field_rows], dyn_halo, tracer_halo)
    advected = tracers.reshape((NTR, LZ) + tracers.shape[1:])
    radius = tracer_halo
    for sub_index in range(NSUB):
        radius -= 1
        advected = advect_tracers(
            advected,
            crop(own_zonal, vel_halo, radius),
            crop(own_merid, vel_halo, radius),
            crop(wet_member_pad, dyn_halo, radius),
        )
    wet_member = crop(wet_member_pad, dyn_halo, 0)
    kinetic = jnp.einsum("ts,szxy->tzxy", rates, advected, precision=lax.Precision.HIGHEST)
    kinetic = kinetic + grazing[:, None, None, None] * (advected[0] * advected[1])[None]
    updated = wet_member[None] * (advected + 0.2 * jnp.exp(0.05 * own_temper)[None] * kinetic)
    light_factor = jnp.exp(-(member_levels + 0.5) / total_levels)
    heating = 0.3 * wet_member * updated[0] * light_factor
    returned = []
    for shift in range(1, groups):
        pairs = [(shift, 0)]
        returned.append(lax.ppermute(heating, "grp", pairs))
    returned = jnp.concatenate(returned, axis=0)
    temper_final = temper + returned
    unused = jnp.zeros((field_rows - dyn_rows, columns, lat_rows), jnp.float32)
    dyn_out = jnp.concatenate([zonal, merid, temper_final, surface[None], unused], axis=0)
    result = jnp.where(member == 0, dyn_out, updated.reshape(field_rows, columns, lat_rows))
    return result[None]


def solution(mesh):
    in_specs = (P("grp", None, "lon", "lat"), P("lon", "lat"), P(), P())
    out_specs = P("grp", None, "lon", "lat")
    return jax.shard_map(body, mesh=mesh, in_specs=in_specs, out_specs=out_specs, check_vma=False)
```

```python
import jax
import jax.numpy as jnp
from jax import lax
from jax.sharding import PartitionSpec as P

LZ = 2
NTR = 20
SECTIONS = 4
NSUB = 4


def exchange(block, width, lat_pos, lat_count):
    lon_count = lax.axis_size("lon")

    def shifted(piece, d_lon, d_lat):
        if d_lat == 0:
            pairs = [(i, (i + d_lon) % lon_count) for i in range(lon_count)]
            return lax.ppermute(piece, "lon", pairs)
        if d_lon == 0:
            pairs = [(j, (j + d_lat) % lat_count) for j in range(lat_count)]
            return lax.ppermute(piece, "lat", pairs)
        pairs = [
            (i * lat_count + j, ((i + d_lon) % lon_count) * lat_count + (j + d_lat) % lat_count)
            for i in range(lon_count)
            for j in range(lat_count)
        ]
        return lax.ppermute(piece, ("lon", "lat"), pairs)

    columns, rows = block.shape[1], block.shape[2]
    low_x, high_x = slice(columns - width, columns), slice(0, width)
    low_y, high_y = slice(rows - width, rows), slice(0, width)
    every = slice(None)
    parts = {}
    for d_lon, xs in ((1, low_x), (0, every), (-1, high_x)):
        for d_lat, ys in ((1, low_y), (0, every), (-1, high_y)):
            if d_lon == 0 and d_lat == 0:
                parts[(d_lon, d_lat)] = block
            else:
                parts[(d_lon, d_lat)] = shifted(block[:, xs, ys], d_lon, d_lat)
    padded = jnp.concatenate(
        [
            jnp.concatenate([parts[(d_lon, 1)], parts[(d_lon, 0)], parts[(d_lon, -1)]], axis=2)
            for d_lon in (1, 0, -1)
        ],
        axis=1,
    )
    length = padded.shape[-1]
    positions = jnp.arange(length)
    lower = (positions < width) & (lat_pos == 0)
    upper = (positions >= length - width) & (lat_pos == lat_count - 1)
    return jnp.where(lower | upper, 0.0, padded)


def crop(array, from_radius, to_radius):
    cut = from_radius - to_radius
    if cut == 0:
        return array
    return array[..., cut : array.shape[-2] - cut, cut : array.shape[-1] - cut]


def center_of(padded):
    return padded[..., 1:-1, 1:-1]


def grad_x(padded):
    return padded[..., 2:, 1:-1] - padded[..., :-2, 1:-1]


def grad_y(padded):
    return padded[..., 1:-1, 2:] - padded[..., 1:-1, :-2]


def laplace(padded):
    return (
        padded[..., 2:, 1:-1]
        + padded[..., :-2, 1:-1]
        + padded[..., 1:-1, 2:]
        + padded[..., 1:-1, :-2]
        - 4.0 * center_of(padded)
    )


def advance_dynamics(zonal_pad, merid_pad, temp_pad, surf_pad, wet_mask, land_mask, coriolis_rows):
    zonal = center_of(zonal_pad)
    merid = center_of(merid_pad)
    temper = center_of(temp_pad)
    surface = center_of(surf_pad)
    divergence = jnp.sum(grad_x(zonal_pad) + grad_y(merid_pad), axis=0)
    zonal_new = wet_mask * (zonal + coriolis_rows * merid - 0.5 * grad_x(surf_pad))
    merid_new = wet_mask * (merid - coriolis_rows * zonal - 0.5 * grad_y(surf_pad))
    surface_new = land_mask * (surface - 0.25 / zonal.shape[0] * divergence)
    temper_new = wet_mask * (
        temper
        - 0.25 * (zonal * grad_x(temp_pad) + merid * grad_y(temp_pad))
        + 0.1 * laplace(temp_pad)
    )
    return (zonal_new, merid_new, temper_new, surface_new)


def advect_tracers(tracer_pad, zonal, merid, wet_mask):
    return wet_mask * (
        center_of(tracer_pad)
        - 0.25 * (zonal * grad_x(tracer_pad) + merid * grad_y(tracer_pad))
        + 0.1 * laplace(tracer_pad)
    )


def section_rows(padded, wet_mask, land_mask, coriolis_rows):
    levels = (padded.shape[0] - 1) // 3
    results = advance_dynamics(
        padded[:levels],
        padded[levels : 2 * levels],
        padded[2 * levels : 3 * levels],
        padded[3 * levels],
        wet_mask,
        land_mask,
        coriolis_rows,
    )
    return jnp.concatenate([results[0], results[1], results[2], results[3][None]], axis=0)


def body(state, depth, rates, grazing):
    groups = lax.axis_size("grp")
    member = lax.axis_index("grp")
    lat_pos = lax.axis_index("lat")
    lat_count = lax.axis_size("lat")
    local = state[0]
    field_rows, columns, lat_rows = local.shape
    total_levels = LZ * (groups - 1)
    dyn_rows = 3 * total_levels + 1
    lat_total = lat_rows * lat_count
    dyn_halo = SECTIONS + NSUB - 1
    tracer_halo = NSUB
    vel_halo = NSUB - 1

    depth_f = depth.astype(jnp.float32)
    block = jnp.concatenate([local, depth_f[None]], axis=0)
    padded = exchange(block, dyn_halo, lat_pos, lat_count)
    depth_pad = padded[field_rows]

    level_index = jnp.arange(total_levels).astype(jnp.float32)[:, None, None]
    wet_pad = (level_index < depth_pad[None]).astype(jnp.float32)
    land_pad = (depth_pad > 0).astype(jnp.float32)
    coord = (lat_pos * lat_rows - dyn_halo + jnp.arange(lat_rows + 2 * dyn_halo)).astype(jnp.float32)
    coriolis_pad = 0.3 * jnp.sin(jnp.pi * (coord + 0.5) / lat_total - jnp.pi / 2)

    current = padded[:dyn_rows]
    radius = dyn_halo
    for section_index in range(SECTIONS):
        radius -= 1
        cut = dyn_halo - radius
        current = section_rows(
            current,
            crop(wet_pad, dyn_halo, radius),
            crop(land_pad, dyn_halo, radius),
            coriolis_pad[cut : coriolis_pad.shape[0] - cut],
        )
    zonal_r = current[:total_levels]
    merid_r = current[total_levels : 2 * total_levels]
    temper_r = current[2 * total_levels : 3 * total_levels]
    zonal = crop(zonal_r, radius, 0)
    merid = crop(merid_r, radius, 0)
    temper = crop(temper_r, radius, 0)
    surface = crop(current[3 * total_levels], radius, 0)

    first_level = jnp.maximum(member - 1, 0) * LZ
    vcols, vrows = zonal_r.shape[-2:]
    forcing = jnp.stack(
        [
            zonal_r.reshape(groups - 1, LZ, vcols, vrows),
            merid_r.reshape(groups - 1, LZ, vcols, vrows),
            temper_r.reshape(groups - 1, LZ, vcols, vrows),
        ],
        axis=1,
    )
    own = forcing[0]
    for shift in range(1, groups):
        pairs = [(0, shift)]
        arrived = lax.ppermute(forcing[shift - 1], "grp", pairs)
        own = jnp.where(member == shift, arrived, own)
    own_zonal = own[0]
    own_merid = own[1]
    own_temper = crop(own[2], vel_halo, 0)

    member_levels = (first_level + jnp.arange(LZ)).astype(jnp.float32)[:, None, None]
    wet_member_pad = (member_levels < depth_pad[None]).astype(jnp.float32)
    tracers = crop(padded[:field_rows], dyn_halo, tracer_halo)
    advected = tracers.reshape((NTR, LZ) + tracers.shape[1:])
    radius = tracer_halo
    for sub_index in range(NSUB):
        radius -= 1
        advected = advect_tracers(
            advected,
            crop(own_zonal, vel_halo, radius),
            crop(own_merid, vel_halo, radius),
            crop(wet_member_pad, dyn_halo, radius),
        )
    wet_member = crop(wet_member_pad, dyn_halo, 0)
    kinetic = jnp.einsum("ts,szxy->tzxy", rates, advected, precision=lax.Precision.HIGHEST)
    kinetic = kinetic + grazing[:, None, None, None] * (advected[0] * advected[1])[None]
    updated = wet_member[None] * (advected + 0.2 * jnp.exp(0.05 * own_temper)[None] * kinetic)
    light_factor = jnp.exp(-(member_levels + 0.5) / total_levels)
    heating = 0.3 * wet_member * updated[0] * light_factor
    returned = []
    for shift in range(1, groups):
        pairs = [(shift, 0)]
        returned.append(lax.ppermute(heating, "grp", pairs))
    returned = jnp.concatenate(returned, axis=0)
    temper_final = temper + returned
    unused = jnp.zeros((field_rows - dyn_rows, columns, lat_rows), jnp.float32)
    dyn_out = jnp.concatenate([zonal, merid, temper_final, surface[None], unused], axis=0)
    result = jnp.where(member == 0, dyn_out, updated.reshape(field_rows, columns, lat_rows))
    return result[None]


def solution(mesh):
    in_specs = (P("grp", None, "lon", "lat"), P("lon", "lat"), P(), P())
    out_specs = P("grp", None, "lon", "lat")
    return jax.shard_map(body, mesh=mesh, in_specs=in_specs, out_specs=out_specs, check_vma=False)
```

```python
import jax
import jax.numpy as jnp
from jax import lax
from jax.sharding import PartitionSpec as P

LZ = 2
NTR = 20
SECTIONS = 4
NSUB = 4


def exchange(block, width, lat_pos, lat_count):
    for axis, dim in (("lon", 1), ("lat", 2)):
        count = lax.axis_size(axis)
        forward = [(i, (i + 1) % count) for i in range(count)]
        backward = [(target, source) for source, target in forward]
        low = lax.ppermute(
            lax.slice_in_dim(block, block.shape[dim] - width, None, axis=dim), axis, forward
        )
        high = lax.ppermute(lax.slice_in_dim(block, 0, width, axis=dim), axis, backward)
        block = jnp.concatenate([low, block, high], axis=dim)
    length = block.shape[-1]
    positions = jnp.arange(length)
    lower = (positions < width) & (lat_pos == 0)
    upper = (positions >= length - width) & (lat_pos == lat_count - 1)
    return jnp.where(lower | upper, 0.0, block)


def crop(array, from_radius, to_radius):
    cut = from_radius - to_radius
    if cut == 0:
        return array
    return array[..., cut : array.shape[-2] - cut, cut : array.shape[-1] - cut]


def center_of(padded):
    return padded[..., 1:-1, 1:-1]


def grad_x(padded):
    return padded[..., 2:, 1:-1] - padded[..., :-2, 1:-1]


def grad_y(padded):
    return padded[..., 1:-1, 2:] - padded[..., 1:-1, :-2]


def laplace(padded):
    return (
        padded[..., 2:, 1:-1]
        + padded[..., :-2, 1:-1]
        + padded[..., 1:-1, 2:]
        + padded[..., 1:-1, :-2]
        - 4.0 * center_of(padded)
    )


def advance_dynamics(zonal_pad, merid_pad, temp_pad, surf_pad, wet_mask, land_mask, coriolis_rows):
    zonal = center_of(zonal_pad)
    merid = center_of(merid_pad)
    temper = center_of(temp_pad)
    surface = center_of(surf_pad)
    divergence = jnp.sum(grad_x(zonal_pad) + grad_y(merid_pad), axis=0)
    zonal_new = wet_mask * (zonal + coriolis_rows * merid - 0.5 * grad_x(surf_pad))
    merid_new = wet_mask * (merid - coriolis_rows * zonal - 0.5 * grad_y(surf_pad))
    surface_new = land_mask * (surface - 0.25 / zonal.shape[0] * divergence)
    temper_new = wet_mask * (
        temper
        - 0.25 * (zonal * grad_x(temp_pad) + merid * grad_y(temp_pad))
        + 0.1 * laplace(temp_pad)
    )
    return (zonal_new, merid_new, temper_new, surface_new)


def advect_tracers(tracer_pad, zonal, merid, wet_mask):
    return wet_mask * (
        center_of(tracer_pad)
        - 0.25 * (zonal * grad_x(tracer_pad) + merid * grad_y(tracer_pad))
        + 0.1 * laplace(tracer_pad)
    )


def section_rows(padded, wet_mask, land_mask, coriolis_rows):
    levels = (padded.shape[0] - 1) // 3
    results = advance_dynamics(
        padded[:levels],
        padded[levels : 2 * levels],
        padded[2 * levels : 3 * levels],
        padded[3 * levels],
        wet_mask,
        land_mask,
        coriolis_rows,
    )
    return jnp.concatenate([results[0], results[1], results[2], results[3][None]], axis=0)


def body(state, depth, rates, grazing):
    groups = lax.axis_size("grp")
    member = lax.axis_index("grp")
    lat_pos = lax.axis_index("lat")
    lat_count = lax.axis_size("lat")
    local = state[0]
    field_rows, columns, lat_rows = local.shape
    total_levels = LZ * (groups - 1)
    dyn_rows = 3 * total_levels + 1
    lat_total = lat_rows * lat_count
    dyn_halo = SECTIONS + NSUB - 1
    tracer_halo = NSUB
    vel_halo = NSUB - 1

    depth_f = depth.astype(jnp.float32)
    block = jnp.concatenate([local, depth_f[None]], axis=0)
    padded = exchange(block, dyn_halo, lat_pos, lat_count)
    depth_pad = padded[field_rows]

    level_index = jnp.arange(total_levels).astype(jnp.float32)[:, None, None]
    wet_pad = (level_index < depth_pad[None]).astype(jnp.float32)
    land_pad = (depth_pad > 0).astype(jnp.float32)
    coord = (lat_pos * lat_rows - dyn_halo + jnp.arange(lat_rows + 2 * dyn_halo)).astype(jnp.float32)
    coriolis_pad = 0.3 * jnp.sin(jnp.pi * (coord + 0.5) / lat_total - jnp.pi / 2)

    current = padded[:dyn_rows]
    radius = dyn_halo
    for section_index in range(SECTIONS):
        radius -= 1
        cut = dyn_halo - radius
        current = section_rows(
            current,
            crop(wet_pad, dyn_halo, radius),
            crop(land_pad, dyn_halo, radius),
            coriolis_pad[cut : coriolis_pad.shape[0] - cut],
        )
    zonal_r = current[:total_levels]
    merid_r = current[total_levels : 2 * total_levels]
    temper_r = current[2 * total_levels : 3 * total_levels]
    zonal = crop(zonal_r, radius, 0)
    merid = crop(merid_r, radius, 0)
    temper = crop(temper_r, radius, 0)
    surface = crop(current[3 * total_levels], radius, 0)

    first_level = jnp.maximum(member - 1, 0) * LZ
    vcols, vrows = zonal_r.shape[-2:]
    forcing = jnp.stack(
        [
            zonal_r.reshape(groups - 1, LZ, vcols, vrows),
            merid_r.reshape(groups - 1, LZ, vcols, vrows),
            temper_r.reshape(groups - 1, LZ, vcols, vrows),
        ],
        axis=1,
    )
    own = forcing[0]
    for shift in range(1, groups):
        pairs = [(0, shift)]
        arrived = lax.ppermute(forcing[shift - 1], "grp", pairs)
        own = jnp.where(member == shift, arrived, own)
    own_zonal = own[0]
    own_merid = own[1]
    own_temper = crop(own[2], vel_halo, 0)

    member_levels = (first_level + jnp.arange(LZ)).astype(jnp.float32)[:, None, None]
    wet_member_pad = (member_levels < depth_pad[None]).astype(jnp.float32)
    tracers = crop(padded[:field_rows], dyn_halo, tracer_halo)
    advected = tracers.reshape((NTR, LZ) + tracers.shape[1:])
    radius = tracer_halo
    for sub_index in range(NSUB):
        radius -= 1
        advected = advect_tracers(
            advected,
            crop(own_zonal, vel_halo, radius),
            crop(own_merid, vel_halo, radius),
            crop(wet_member_pad, dyn_halo, radius),
        )
    wet_member = crop(wet_member_pad, dyn_halo, 0)
    kinetic = grazing[:, None, None, None] * (advected[0] * advected[1])[None]
    for source in range(NTR):
        kinetic = kinetic + rates[:, source, None, None, None] * advected[source][None]
    updated = wet_member[None] * (advected + 0.2 * jnp.exp(0.05 * own_temper)[None] * kinetic)
    light_factor = jnp.exp(-(member_levels + 0.5) / total_levels)
    heating = 0.3 * wet_member * updated[0] * light_factor
    returned = []
    for shift in range(1, groups):
        pairs = [(shift, 0)]
        returned.append(lax.ppermute(heating, "grp", pairs))
    returned = jnp.concatenate(returned, axis=0)
    temper_final = temper + returned
    unused = jnp.zeros((field_rows - dyn_rows, columns, lat_rows), jnp.float32)
    dyn_out = jnp.concatenate([zonal, merid, temper_final, surface[None], unused], axis=0)
    result = jnp.where(member == 0, dyn_out, updated.reshape(field_rows, columns, lat_rows))
    return result[None]


def solution(mesh):
    in_specs = (P("grp", None, "lon", "lat"), P("lon", "lat"), P(), P())
    out_specs = P("grp", None, "lon", "lat")
    return jax.shard_map(body, mesh=mesh, in_specs=in_specs, out_specs=out_specs, check_vma=False)
```

```python
import jax
import jax.numpy as jnp
from jax import lax
from jax.sharding import PartitionSpec as P

LZ = 2
NTR = 20
SECTIONS = 4
NSUB = 4


def exchange(block, width, lat_pos, lat_count):
    for axis, dim in (("lon", 1), ("lat", 2)):
        count = lax.axis_size(axis)
        forward = [(i, (i + 1) % count) for i in range(count)]
        backward = [(target, source) for source, target in forward]
        low = lax.ppermute(
            lax.slice_in_dim(block, block.shape[dim] - width, None, axis=dim), axis, forward
        )
        high = lax.ppermute(lax.slice_in_dim(block, 0, width, axis=dim), axis, backward)
        block = jnp.concatenate([low, block, high], axis=dim)
    length = block.shape[-1]
    positions = jnp.arange(length)
    lower = (positions < width) & (lat_pos == 0)
    upper = (positions >= length - width) & (lat_pos == lat_count - 1)
    return jnp.where(lower | upper, 0.0, block)


def crop(array, from_radius, to_radius):
    cut = from_radius - to_radius
    if cut == 0:
        return array
    return array[..., cut : array.shape[-2] - cut, cut : array.shape[-1] - cut]


def center_of(padded):
    return padded[..., 1:-1, 1:-1]


def grad_x(padded):
    return padded[..., 2:, 1:-1] - padded[..., :-2, 1:-1]


def grad_y(padded):
    return padded[..., 1:-1, 2:] - padded[..., 1:-1, :-2]


def laplace(padded):
    return (
        padded[..., 2:, 1:-1]
        + padded[..., :-2, 1:-1]
        + padded[..., 1:-1, 2:]
        + padded[..., 1:-1, :-2]
        - 4.0 * center_of(padded)
    )


def advance_dynamics(zonal_pad, merid_pad, temp_pad, surf_pad, wet_mask, land_mask, coriolis_rows):
    zonal = center_of(zonal_pad)
    merid = center_of(merid_pad)
    temper = center_of(temp_pad)
    surface = center_of(surf_pad)
    divergence = jnp.sum(grad_x(zonal_pad) + grad_y(merid_pad), axis=0)
    zonal_new = wet_mask * (zonal + coriolis_rows * merid - 0.5 * grad_x(surf_pad))
    merid_new = wet_mask * (merid - coriolis_rows * zonal - 0.5 * grad_y(surf_pad))
    surface_new = land_mask * (surface - 0.25 / zonal.shape[0] * divergence)
    temper_new = wet_mask * (
        temper
        - 0.25 * (zonal * grad_x(temp_pad) + merid * grad_y(temp_pad))
        + 0.1 * laplace(temp_pad)
    )
    return (zonal_new, merid_new, temper_new, surface_new)


def advect_tracers(tracer_pad, zonal, merid, wet_mask):
    return wet_mask * (
        center_of(tracer_pad)
        - 0.25 * (zonal * grad_x(tracer_pad) + merid * grad_y(tracer_pad))
        + 0.1 * laplace(tracer_pad)
    )


def section_rows(padded, wet_mask, land_mask, coriolis_rows):
    levels = (padded.shape[0] - 1) // 3
    results = advance_dynamics(
        padded[:levels],
        padded[levels : 2 * levels],
        padded[2 * levels : 3 * levels],
        padded[3 * levels],
        wet_mask,
        land_mask,
        coriolis_rows,
    )
    return jnp.concatenate([results[0], results[1], results[2], results[3][None]], axis=0)


def body(state, depth, rates, grazing):
    groups = lax.axis_size("grp")
    member = lax.axis_index("grp")
    lat_pos = lax.axis_index("lat")
    lat_count = lax.axis_size("lat")
    local = state[0]
    field_rows, columns, lat_rows = local.shape
    total_levels = LZ * (groups - 1)
    dyn_rows = 3 * total_levels + 1
    lat_total = lat_rows * lat_count
    dyn_halo = SECTIONS + NSUB - 1
    tracer_halo = NSUB
    vel_halo = NSUB - 1

    depth_f = depth.astype(jnp.float32)
    block = jnp.concatenate([local, depth_f[None]], axis=0)
    padded = exchange(block, dyn_halo, lat_pos, lat_count)
    depth_pad = padded[field_rows]

    level_index = jnp.arange(total_levels).astype(jnp.float32)[:, None, None]
    wet_pad = (level_index < depth_pad[None]).astype(jnp.float32)
    land_pad = (depth_pad > 0).astype(jnp.float32)
    coord = (lat_pos * lat_rows - dyn_halo + jnp.arange(lat_rows + 2 * dyn_halo)).astype(jnp.float32)
    coriolis_pad = 0.3 * jnp.sin(jnp.pi * (coord + 0.5) / lat_total - jnp.pi / 2)

    current = padded[:dyn_rows]
    radius = dyn_halo
    for section_index in range(SECTIONS):
        radius -= 1
        cut = dyn_halo - radius
        current = section_rows(
            current,
            crop(wet_pad, dyn_halo, radius),
            crop(land_pad, dyn_halo, radius),
            coriolis_pad[cut : coriolis_pad.shape[0] - cut],
        )
    zonal_r = current[:total_levels]
    merid_r = current[total_levels : 2 * total_levels]
    temper_r = current[2 * total_levels : 3 * total_levels]
    zonal = crop(zonal_r, radius, 0)
    merid = crop(merid_r, radius, 0)
    temper = crop(temper_r, radius, 0)
    surface = crop(current[3 * total_levels], radius, 0)

    first_level = jnp.maximum(member - 1, 0) * LZ
    vcols, vrows = zonal_r.shape[-2:]
    own = None
    for shift in range(1, groups):
        levels = slice((shift - 1) * LZ, shift * LZ)
        payload = jnp.concatenate(
            [zonal_r[levels].reshape(-1), merid_r[levels].reshape(-1), temper[levels].reshape(-1)]
        )
        arrived = lax.ppermute(payload, "grp", [(0, shift)])
        own = arrived if own is None else jnp.where(member == shift, arrived, own)
    vel_size = LZ * vcols * vrows
    own_zonal = own[:vel_size].reshape(LZ, vcols, vrows)
    own_merid = own[vel_size : 2 * vel_size].reshape(LZ, vcols, vrows)
    own_temper = own[2 * vel_size :].reshape(LZ, columns, lat_rows)

    member_levels = (first_level + jnp.arange(LZ)).astype(jnp.float32)[:, None, None]
    wet_member_pad = (member_levels < depth_pad[None]).astype(jnp.float32)
    tracers = crop(padded[:field_rows], dyn_halo, tracer_halo)
    advected = tracers.reshape((NTR, LZ) + tracers.shape[1:])
    radius = tracer_halo
    for sub_index in range(NSUB):
        radius -= 1
        advected = advect_tracers(
            advected,
            crop(own_zonal, vel_halo, radius),
            crop(own_merid, vel_halo, radius),
            crop(wet_member_pad, dyn_halo, radius),
        )
    wet_member = crop(wet_member_pad, dyn_halo, 0)
    kinetic = grazing[:, None, None, None] * (advected[0] * advected[1])[None]
    for source in range(NTR):
        kinetic = kinetic + rates[:, source, None, None, None] * advected[source][None]
    updated = wet_member[None] * (advected + 0.2 * jnp.exp(0.05 * own_temper)[None] * kinetic)
    light_factor = jnp.exp(-(member_levels + 0.5) / total_levels)
    heating = 0.3 * wet_member * updated[0] * light_factor
    returned = []
    for shift in range(1, groups):
        pairs = [(shift, 0)]
        returned.append(lax.ppermute(heating, "grp", pairs))
    returned = jnp.concatenate(returned, axis=0)
    temper_final = temper + returned
    unused = jnp.zeros((field_rows - dyn_rows, columns, lat_rows), jnp.float32)
    dyn_out = jnp.concatenate([zonal, merid, temper_final, surface[None], unused], axis=0)
    result = jnp.where(member == 0, dyn_out, updated.reshape(field_rows, columns, lat_rows))
    return result[None]


def solution(mesh):
    in_specs = (P("grp", None, "lon", "lat"), P("lon", "lat"), P(), P())
    out_specs = P("grp", None, "lon", "lat")
    return jax.shard_map(body, mesh=mesh, in_specs=in_specs, out_specs=out_specs, check_vma=False)
```

```python
import jax
import jax.numpy as jnp
from jax import lax
from jax.sharding import PartitionSpec as P


LZ = 2
NTR = 20
SECTIONS = 4
NSUB = 4


def exchange(block, width, lat_pos, lat_count):
    for axis, dim in (("lon", 1), ("lat", 2)):
        count = lax.axis_size(axis)
        forward = [(i, (i + 1) % count) for i in range(count)]
        backward = [(target, source) for source, target in forward]
        low = lax.ppermute(
            lax.slice_in_dim(block, block.shape[dim] - width, None, axis=dim), axis, forward
        )
        high = lax.ppermute(lax.slice_in_dim(block, 0, width, axis=dim), axis, backward)
        block = jnp.concatenate([low, block, high], axis=dim)
    length = block.shape[-1]
    positions = jnp.arange(length)
    lower = (positions < width) & (lat_pos == 0)
    upper = (positions >= length - width) & (lat_pos == lat_count - 1)
    return jnp.where(lower | upper, 0.0, block)


def crop(array, from_radius, to_radius):
    cut = from_radius - to_radius
    if cut == 0:
        return array
    return array[..., cut : array.shape[-2] - cut, cut : array.shape[-1] - cut]


def center_of(padded):
    return padded[..., 1:-1, 1:-1]


def grad_x(padded):
    return padded[..., 2:, 1:-1] - padded[..., :-2, 1:-1]


def grad_y(padded):
    return padded[..., 1:-1, 2:] - padded[..., 1:-1, :-2]


def laplace(padded):
    return (
        padded[..., 2:, 1:-1]
        + padded[..., :-2, 1:-1]
        + padded[..., 1:-1, 2:]
        + padded[..., 1:-1, :-2]
        - 4.0 * center_of(padded)
    )


def advance_dynamics(zonal_pad, merid_pad, temp_pad, surf_pad, wet_mask, land_mask, coriolis_rows):
    zonal = center_of(zonal_pad)
    merid = center_of(merid_pad)
    temper = center_of(temp_pad)
    surface = center_of(surf_pad)
    divergence = jnp.sum(grad_x(zonal_pad) + grad_y(merid_pad), axis=0)
    zonal_new = wet_mask * (zonal + coriolis_rows * merid - 0.5 * grad_x(surf_pad))
    merid_new = wet_mask * (merid - coriolis_rows * zonal - 0.5 * grad_y(surf_pad))
    surface_new = land_mask * (surface - 0.25 / zonal.shape[0] * divergence)
    temper_new = wet_mask * (
        temper
        - 0.25 * (zonal * grad_x(temp_pad) + merid * grad_y(temp_pad))
        + 0.1 * laplace(temp_pad)
    )
    return (zonal_new, merid_new, temper_new, surface_new)


def advect_tracers(tracer_pad, zonal, merid, wet_mask):
    return wet_mask * (
        center_of(tracer_pad)
        - 0.25 * (zonal * grad_x(tracer_pad) + merid * grad_y(tracer_pad))
        + 0.1 * laplace(tracer_pad)
    )


def section_rows(padded, wet_mask, land_mask, coriolis_rows):
    levels = (padded.shape[0] - 1) // 3
    results = advance_dynamics(
        padded[:levels],
        padded[levels : 2 * levels],
        padded[2 * levels : 3 * levels],
        padded[3 * levels],
        wet_mask,
        land_mask,
        coriolis_rows,
    )
    return jnp.concatenate([results[0], results[1], results[2], results[3][None]], axis=0)


def step_body(state, depth, rates, grazing):
    groups = lax.axis_size("grp")
    member = lax.axis_index("grp")
    lat_pos = lax.axis_index("lat")
    lat_count = lax.axis_size("lat")
    local = state[0]
    field_rows, columns, lat_rows = local.shape
    total_levels = LZ * (groups - 1)
    dyn_rows = 3 * total_levels + 1
    lat_total = lat_rows * lat_count
    dyn_halo = SECTIONS + NSUB - 1
    tracer_halo = NSUB
    vel_halo = NSUB - 1

    depth_f = depth.astype(jnp.float32)
    block = jnp.concatenate([local, depth_f[None]], axis=0)
    padded = exchange(block, dyn_halo, lat_pos, lat_count)
    depth_pad = padded[field_rows]

    level_index = jnp.arange(total_levels).astype(jnp.float32)[:, None, None]
    wet_pad = (level_index < depth_pad[None]).astype(jnp.float32)
    land_pad = (depth_pad > 0).astype(jnp.float32)
    coord = (lat_pos * lat_rows - dyn_halo + jnp.arange(lat_rows + 2 * dyn_halo)).astype(jnp.float32)
    coriolis_pad = 0.3 * jnp.sin(jnp.pi * (coord + 0.5) / lat_total - jnp.pi / 2)

    current = padded[:dyn_rows]
    radius = dyn_halo
    for _ in range(SECTIONS):
        radius -= 1
        cut = dyn_halo - radius
        current = section_rows(
            current,
            crop(wet_pad, dyn_halo, radius),
            crop(land_pad, dyn_halo, radius),
            coriolis_pad[cut : coriolis_pad.shape[0] - cut],
        )
    zonal_r = current[:total_levels]
    merid_r = current[total_levels : 2 * total_levels]
    temper_r = current[2 * total_levels : 3 * total_levels]
    zonal = crop(zonal_r, radius, 0)
    merid = crop(merid_r, radius, 0)
    temper = crop(temper_r, radius, 0)
    surface = crop(current[3 * total_levels], radius, 0)

    first_level = jnp.maximum(member - 1, 0) * LZ
    own_wind = None
    own_temper = None
    for shift in range(1, groups):
        levels = slice((shift - 1) * LZ, shift * LZ)
        wind = jnp.stack([zonal_r[levels], merid_r[levels]])
        arrived = lax.ppermute(wind, "grp", [(0, shift)])
        own_wind = arrived if own_wind is None else jnp.where(member == shift, arrived, own_wind)
    for shift in range(1, groups):
        levels = slice((shift - 1) * LZ, shift * LZ)
        arrived = lax.ppermute(temper[levels], "grp", [(0, shift)])
        own_temper = arrived if own_temper is None else jnp.where(member == shift, arrived, own_temper)
    own_zonal = own_wind[0]
    own_merid = own_wind[1]

    member_levels = (first_level + jnp.arange(LZ)).astype(jnp.float32)[:, None, None]
    wet_member_pad = (member_levels < depth_pad[None]).astype(jnp.float32)
    tracers = crop(padded[:field_rows], dyn_halo, tracer_halo)
    advected = tracers.reshape((NTR, LZ) + tracers.shape[1:])
    radius = tracer_halo
    for _ in range(NSUB):
        radius -= 1
        advected = advect_tracers(
            advected,
            crop(own_zonal, vel_halo, radius),
            crop(own_merid, vel_halo, radius),
            crop(wet_member_pad, dyn_halo, radius),
        )
    wet_member = crop(wet_member_pad, dyn_halo, 0)
    kinetic = grazing[:, None, None, None] * (advected[0] * advected[1])[None]
    for source in range(NTR):
        kinetic = kinetic + rates[:, source, None, None, None] * advected[source][None]
    updated = wet_member[None] * (advected + 0.2 * jnp.exp(0.05 * own_temper)[None] * kinetic)
    light_factor = jnp.exp(-(member_levels + 0.5) / total_levels)
    heating = 0.3 * wet_member * updated[0] * light_factor
    returned = []
    for shift in range(1, groups):
        pairs = [(shift, 0)]
        returned.append(lax.ppermute(heating, "grp", pairs))
    returned = jnp.concatenate(returned, axis=0)
    temper_final = temper + returned
    unused = jnp.zeros((field_rows - dyn_rows, columns, lat_rows), jnp.float32)
    dyn_out = jnp.concatenate([zonal, merid, temper_final, surface[None], unused], axis=0)
    result = jnp.where(member == 0, dyn_out, updated.reshape(field_rows, columns, lat_rows))
    return result[None]


def solution(mesh):
    in_specs = (P("grp", None, "lon", "lat"), P("lon", "lat"), P(), P())
    out_specs = P("grp", None, "lon", "lat")
    return jax.shard_map(step_body, mesh=mesh, in_specs=in_specs, out_specs=out_specs, check_vma=False)
```

```python
import jax
import jax.numpy as jnp
from jax import lax
from jax.sharding import PartitionSpec as P

LZ = 2
NTR = 20
SECTIONS = 4
NSUB = 4


def exchange(block, width, lat_pos, lat_count):
    count = lax.axis_size("lon")
    forward = [(i, (i + 1) % count) for i in range(count)]
    backward = [(target, source) for source, target in forward]
    low = lax.ppermute(lax.slice_in_dim(block, block.shape[1] - width, None, axis=1), "lon", forward)
    high = lax.ppermute(lax.slice_in_dim(block, 0, width, axis=1), "lon", backward)
    block = jnp.concatenate([low, block, high], axis=1)
    to_up = lax.slice_in_dim(block, block.shape[2] - width, None, axis=2)
    to_down = lax.slice_in_dim(block, 0, width, axis=2)
    chunk = jnp.arange(lat_count)[:, None, None, None]
    up = (lat_pos + 1) % lat_count
    down = (lat_pos + lat_count - 1) % lat_count
    outgoing = jnp.where(chunk == up, to_up[None], jnp.where(chunk == down, to_down[None], 0.0))
    received = lax.all_to_all(outgoing, "lat", split_axis=0, concat_axis=0, tiled=True)
    low = jnp.sum(jnp.where(chunk == down, received, 0.0), axis=0)
    high = jnp.sum(jnp.where(chunk == up, received, 0.0), axis=0)
    block = jnp.concatenate([low, block, high], axis=2)
    length = block.shape[-1]
    positions = jnp.arange(length)
    lower = (positions < width) & (lat_pos == 0)
    upper = (positions >= length - width) & (lat_pos == lat_count - 1)
    return jnp.where(lower | upper, 0.0, block)


def crop(array, from_radius, to_radius):
    cut = from_radius - to_radius
    if cut == 0:
        return array
    return array[..., cut : array.shape[-2] - cut, cut : array.shape[-1] - cut]


def center_of(padded):
    return padded[..., 1:-1, 1:-1]


def grad_x(padded):
    return padded[..., 2:, 1:-1] - padded[..., :-2, 1:-1]


def grad_y(padded):
    return padded[..., 1:-1, 2:] - padded[..., 1:-1, :-2]


def laplace(padded):
    return (
        padded[..., 2:, 1:-1]
        + padded[..., :-2, 1:-1]
        + padded[..., 1:-1, 2:]
        + padded[..., 1:-1, :-2]
        - 4.0 * center_of(padded)
    )


def advance_dynamics(zonal_pad, merid_pad, temp_pad, surf_pad, wet_mask, land_mask, coriolis_rows):
    zonal = center_of(zonal_pad)
    merid = center_of(merid_pad)
    temper = center_of(temp_pad)
    surface = center_of(surf_pad)
    divergence = jnp.sum(grad_x(zonal_pad) + grad_y(merid_pad), axis=0)
    zonal_new = wet_mask * (zonal + coriolis_rows * merid - 0.5 * grad_x(surf_pad))
    merid_new = wet_mask * (merid - coriolis_rows * zonal - 0.5 * grad_y(surf_pad))
    surface_new = land_mask * (surface - 0.25 / zonal.shape[0] * divergence)
    temper_new = wet_mask * (
        temper
        - 0.25 * (zonal * grad_x(temp_pad) + merid * grad_y(temp_pad))
        + 0.1 * laplace(temp_pad)
    )
    return (zonal_new, merid_new, temper_new, surface_new)


def advect_tracers(tracer_pad, zonal, merid, wet_mask):
    return wet_mask * (
        center_of(tracer_pad)
        - 0.25 * (zonal * grad_x(tracer_pad) + merid * grad_y(tracer_pad))
        + 0.1 * laplace(tracer_pad)
    )


def section_rows(padded, wet_mask, land_mask, coriolis_rows):
    levels = (padded.shape[0] - 1) // 3
    results = advance_dynamics(
        padded[:levels],
        padded[levels : 2 * levels],
        padded[2 * levels : 3 * levels],
        padded[3 * levels],
        wet_mask,
        land_mask,
        coriolis_rows,
    )
    return jnp.concatenate([results[0], results[1], results[2], results[3][None]], axis=0)


def body(state, depth, rates, grazing):
    groups = lax.axis_size("grp")
    member = lax.axis_index("grp")
    lat_pos = lax.axis_index("lat")
    lat_count = lax.axis_size("lat")
    local = state[0]
    field_rows, columns, lat_rows = local.shape
    total_levels = LZ * (groups - 1)
    dyn_rows = 3 * total_levels + 1
    lat_total = lat_rows * lat_count
    dyn_halo = SECTIONS + NSUB - 1
    tracer_halo = NSUB
    vel_halo = NSUB - 1

    depth_f = depth.astype(jnp.float32)
    block = jnp.concatenate([local, depth_f[None]], axis=0)
    padded = exchange(block, dyn_halo, lat_pos, lat_count)
    depth_pad = padded[field_rows]

    level_index = jnp.arange(total_levels).astype(jnp.float32)[:, None, None]
    wet_pad = (level_index < depth_pad[None]).astype(jnp.float32)
    land_pad = (depth_pad > 0).astype(jnp.float32)
    coord = (lat_pos * lat_rows - dyn_halo + jnp.arange(lat_rows + 2 * dyn_halo)).astype(jnp.float32)
    coriolis_pad = 0.3 * jnp.sin(jnp.pi * (coord + 0.5) / lat_total - jnp.pi / 2)

    current = padded[:dyn_rows]
    radius = dyn_halo
    for section_index in range(SECTIONS):
        radius -= 1
        cut = dyn_halo - radius
        current = section_rows(
            current,
            crop(wet_pad, dyn_halo, radius),
            crop(land_pad, dyn_halo, radius),
            coriolis_pad[cut : coriolis_pad.shape[0] - cut],
        )
    zonal_r = current[:total_levels]
    merid_r = current[total_levels : 2 * total_levels]
    temper_r = current[2 * total_levels : 3 * total_levels]
    zonal = crop(zonal_r, radius, 0)
    merid = crop(merid_r, radius, 0)
    temper = crop(temper_r, radius, 0)
    surface = crop(current[3 * total_levels], radius, 0)

    first_level = jnp.maximum(member - 1, 0) * LZ
    vcols, vrows = zonal_r.shape[-2:]
    forcing = jnp.stack(
        [
            zonal_r.reshape(groups - 1, LZ, vcols, vrows),
            merid_r.reshape(groups - 1, LZ, vcols, vrows),
            temper_r.reshape(groups - 1, LZ, vcols, vrows),
        ],
        axis=1,
    )
    own = forcing[0]
    for shift in range(1, groups):
        pairs = [(0, shift)]
        arrived = lax.ppermute(forcing[shift - 1], "grp", pairs)
        own = jnp.where(member == shift, arrived, own)
    own_zonal = own[0]
    own_merid = own[1]
    own_temper = crop(own[2], vel_halo, 0)

    member_levels = (first_level + jnp.arange(LZ)).astype(jnp.float32)[:, None, None]
    wet_member_pad = (member_levels < depth_pad[None]).astype(jnp.float32)
    tracers = crop(padded[:field_rows], dyn_halo, tracer_halo)
    advected = tracers.reshape((NTR, LZ) + tracers.shape[1:])
    radius = tracer_halo
    for sub_index in range(NSUB):
        radius -= 1
        advected = advect_tracers(
            advected,
            crop(own_zonal, vel_halo, radius),
            crop(own_merid, vel_halo, radius),
            crop(wet_member_pad, dyn_halo, radius),
        )
    wet_member = crop(wet_member_pad, dyn_halo, 0)
    kinetic = grazing[:, None, None, None] * (advected[0] * advected[1])[None]
    for source in range(NTR):
        kinetic = kinetic + rates[:, source, None, None, None] * advected[source][None]
    updated = wet_member[None] * (advected + 0.2 * jnp.exp(0.05 * own_temper)[None] * kinetic)
    light_factor = jnp.exp(-(member_levels + 0.5) / total_levels)
    heating = 0.3 * wet_member * updated[0] * light_factor
    returned = []
    for shift in range(1, groups):
        pairs = [(shift, 0)]
        returned.append(lax.ppermute(heating, "grp", pairs))
    returned = jnp.concatenate(returned, axis=0)
    temper_final = temper + returned
    unused = jnp.zeros((field_rows - dyn_rows, columns, lat_rows), jnp.float32)
    dyn_out = jnp.concatenate([zonal, merid, temper_final, surface[None], unused], axis=0)
    result = jnp.where(member == 0, dyn_out, updated.reshape(field_rows, columns, lat_rows))
    return result[None]


def solution(mesh):
    in_specs = (P("grp", None, "lon", "lat"), P("lon", "lat"), P(), P())
    out_specs = P("grp", None, "lon", "lat")
    return jax.shard_map(body, mesh=mesh, in_specs=in_specs, out_specs=out_specs, check_vma=False)
```

```python
import jax
import jax.numpy as jnp
from jax import lax
from jax.sharding import PartitionSpec as P

LZ = 2
NTR = 20
SECTIONS = 4
NSUB = 4


def exchange(block, width, lat_pos, lat_count):
    for axis, dim in (("lon", 1), ("lat", 2)):
        count = lax.axis_size(axis)
        forward = [(i, (i + 1) % count) for i in range(count)]
        backward = [(target, source) for source, target in forward]
        low = lax.ppermute(
            lax.slice_in_dim(block, block.shape[dim] - width, None, axis=dim), axis, forward
        )
        high = lax.ppermute(lax.slice_in_dim(block, 0, width, axis=dim), axis, backward)
        block = jnp.concatenate([low, block, high], axis=dim)
    length = block.shape[-1]
    positions = jnp.arange(length)
    lower = (positions < width) & (lat_pos == 0)
    upper = (positions >= length - width) & (lat_pos == lat_count - 1)
    return jnp.where(lower | upper, 0.0, block)


def crop(array, from_radius, to_radius):
    cut = from_radius - to_radius
    if cut == 0:
        return array
    return array[..., cut : array.shape[-2] - cut, cut : array.shape[-1] - cut]


def center_of(padded):
    return padded[..., 1:-1, 1:-1]


def grad_x(padded):
    return padded[..., 2:, 1:-1] - padded[..., :-2, 1:-1]


def grad_y(padded):
    return padded[..., 1:-1, 2:] - padded[..., 1:-1, :-2]


def laplace(padded):
    return (
        padded[..., 2:, 1:-1]
        + padded[..., :-2, 1:-1]
        + padded[..., 1:-1, 2:]
        + padded[..., 1:-1, :-2]
        - 4.0 * center_of(padded)
    )


def advance_dynamics(zonal_pad, merid_pad, temp_pad, surf_pad, wet_mask, land_mask, coriolis_rows):
    zonal = center_of(zonal_pad)
    merid = center_of(merid_pad)
    temper = center_of(temp_pad)
    surface = center_of(surf_pad)
    divergence = jnp.sum(grad_x(zonal_pad) + grad_y(merid_pad), axis=0)
    zonal_new = wet_mask * (zonal + coriolis_rows * merid - 0.5 * grad_x(surf_pad))
    merid_new = wet_mask * (merid - coriolis_rows * zonal - 0.5 * grad_y(surf_pad))
    surface_new = land_mask * (surface - 0.25 / zonal.shape[0] * divergence)
    temper_new = wet_mask * (
        temper
        - 0.25 * (zonal * grad_x(temp_pad) + merid * grad_y(temp_pad))
        + 0.1 * laplace(temp_pad)
    )
    return (zonal_new, merid_new, temper_new, surface_new)


def advect_tracers(tracer_pad, zonal, merid, wet_mask):
    return wet_mask * (
        center_of(tracer_pad)
        - 0.25 * (zonal * grad_x(tracer_pad) + merid * grad_y(tracer_pad))
        + 0.1 * laplace(tracer_pad)
    )


def section_rows(padded, wet_mask, land_mask, coriolis_rows):
    levels = (padded.shape[0] - 1) // 3
    results = advance_dynamics(
        padded[:levels],
        padded[levels : 2 * levels],
        padded[2 * levels : 3 * levels],
        padded[3 * levels],
        wet_mask,
        land_mask,
        coriolis_rows,
    )
    return jnp.concatenate([results[0], results[1], results[2], results[3][None]], axis=0)


def body(state, depth, rates, grazing):
    groups = lax.axis_size("grp")
    member = lax.axis_index("grp")
    lat_pos = lax.axis_index("lat")
    lat_count = lax.axis_size("lat")
    local = state[0]
    field_rows, columns, lat_rows = local.shape
    total_levels = LZ * (groups - 1)
    dyn_rows = 3 * total_levels + 1
    lat_total = lat_rows * lat_count
    dyn_halo = SECTIONS + NSUB - 1
    tracer_halo = NSUB
    vel_halo = NSUB - 1

    depth_f = depth.astype(jnp.float32)
    block = jnp.concatenate([local, depth_f[None]], axis=0)
    padded = exchange(block, dyn_halo, lat_pos, lat_count)
    depth_pad = padded[field_rows]

    level_index = jnp.arange(total_levels).astype(jnp.float32)[:, None, None]
    wet_pad = (level_index < depth_pad[None]).astype(jnp.float32)
    land_pad = (depth_pad > 0).astype(jnp.float32)
    coord = (lat_pos * lat_rows - dyn_halo + jnp.arange(lat_rows + 2 * dyn_halo)).astype(jnp.float32)
    coriolis_pad = 0.3 * jnp.sin(jnp.pi * (coord + 0.5) / lat_total - jnp.pi / 2)

    def dynamics(fields, wet_pad, land_pad, coriolis_pad):
        radius = dyn_halo
        for section_index in range(SECTIONS):
            radius -= 1
            cut = dyn_halo - radius
            fields = section_rows(
                fields,
                crop(wet_pad, dyn_halo, radius),
                crop(land_pad, dyn_halo, radius),
                coriolis_pad[cut : coriolis_pad.shape[0] - cut],
            )
        return fields

    def no_dynamics(fields, wet_pad, land_pad, coriolis_pad):
        return jnp.zeros(fields.shape[:1] + crop(fields, dyn_halo, vel_halo).shape[1:], fields.dtype)

    current = lax.cond(
        member == 0, dynamics, no_dynamics, padded[:dyn_rows], wet_pad, land_pad, coriolis_pad
    )
    radius = vel_halo
    zonal_r = current[:total_levels]
    merid_r = current[total_levels : 2 * total_levels]
    temper_r = current[2 * total_levels : 3 * total_levels]
    zonal = crop(zonal_r, radius, 0)
    merid = crop(merid_r, radius, 0)
    temper = crop(temper_r, radius, 0)
    surface = crop(current[3 * total_levels], radius, 0)

    first_level = jnp.maximum(member - 1, 0) * LZ
    vcols, vrows = zonal_r.shape[-2:]
    forcing = jnp.stack(
        [
            zonal_r.reshape(groups - 1, LZ, vcols, vrows),
            merid_r.reshape(groups - 1, LZ, vcols, vrows),
            temper_r.reshape(groups - 1, LZ, vcols, vrows),
        ],
        axis=1,
    )
    own = forcing[0]
    for shift in range(1, groups):
        pairs = [(0, shift)]
        arrived = lax.ppermute(forcing[shift - 1], "grp", pairs)
        own = jnp.where(member == shift, arrived, own)
    own_zonal = own[0]
    own_merid = own[1]
    own_temper = crop(own[2], vel_halo, 0)

    member_levels = (first_level + jnp.arange(LZ)).astype(jnp.float32)[:, None, None]
    wet_member_pad = (member_levels < depth_pad[None]).astype(jnp.float32)
    tracers = crop(padded[:field_rows], dyn_halo, tracer_halo)
    light_factor = jnp.exp(-(member_levels + 0.5) / total_levels)

    def transport(tracers, own_zonal, own_merid, own_temper, wet_member_pad, rates, grazing):
        advected = tracers.reshape((NTR, LZ) + tracers.shape[1:])
        radius = tracer_halo
        for sub_index in range(NSUB):
            radius -= 1
            advected = advect_tracers(
                advected,
                crop(own_zonal, vel_halo, radius),
                crop(own_merid, vel_halo, radius),
                crop(wet_member_pad, dyn_halo, radius),
            )
        wet_member = crop(wet_member_pad, dyn_halo, 0)
        kinetic = grazing[:, None, None, None] * (advected[0] * advected[1])[None]
        for source in range(NTR):
            kinetic = kinetic + rates[:, source, None, None, None] * advected[source][None]
        updated = wet_member[None] * (advected + 0.2 * jnp.exp(0.05 * own_temper)[None] * kinetic)
        heating = 0.3 * wet_member * updated[0] * light_factor
        return updated, heating

    def no_transport(tracers, own_zonal, own_merid, own_temper, wet_member_pad, rates, grazing):
        return (
            jnp.zeros((NTR, LZ, columns, lat_rows), jnp.float32),
            jnp.zeros((LZ, columns, lat_rows), jnp.float32),
        )

    updated, heating = lax.cond(
        member == 0,
        no_transport,
        transport,
        tracers,
        own_zonal,
        own_merid,
        own_temper,
        wet_member_pad,
        rates,
        grazing,
    )
    returned = []
    for shift in range(1, groups):
        pairs = [(shift, 0)]
        returned.append(lax.ppermute(heating, "grp", pairs))
    returned = jnp.concatenate(returned, axis=0)
    temper_final = temper + returned
    unused = jnp.zeros((field_rows - dyn_rows, columns, lat_rows), jnp.float32)
    dyn_out = jnp.concatenate([zonal, merid, temper_final, surface[None], unused], axis=0)
    result = jnp.where(member == 0, dyn_out, updated.reshape(field_rows, columns, lat_rows))
    return result[None]


def solution(mesh):
    in_specs = (P("grp", None, "lon", "lat"), P("lon", "lat"), P(), P())
    out_specs = P("grp", None, "lon", "lat")
    return jax.shard_map(body, mesh=mesh, in_specs=in_specs, out_specs=out_specs, check_vma=False)
```

```python
import jax
import jax.numpy as jnp
from jax import lax
from jax.sharding import PartitionSpec as P

LZ = 2
NTR = 20
SECTIONS = 4
NSUB = 4


def exchange(block, width, lat_pos, lat_count):
    for axis, dim in (("lon", 1), ("lat", 2)):
        count = lax.axis_size(axis)
        forward = [(i, (i + 1) % count) for i in range(count)]
        backward = [(target, source) for source, target in forward]
        low = lax.ppermute(
            lax.slice_in_dim(block, block.shape[dim] - width, None, axis=dim), axis, forward
        )
        high = lax.ppermute(lax.slice_in_dim(block, 0, width, axis=dim), axis, backward)
        block = jnp.concatenate([low, block, high], axis=dim)
    length = block.shape[-1]
    positions = jnp.arange(length)
    lower = (positions < width) & (lat_pos == 0)
    upper = (positions >= length - width) & (lat_pos == lat_count - 1)
    return jnp.where(lower | upper, 0.0, block)


def crop(array, from_radius, to_radius):
    cut = from_radius - to_radius
    if cut == 0:
        return array
    return array[..., cut : array.shape[-2] - cut, cut : array.shape[-1] - cut]


def center_of(padded):
    return padded[..., 1:-1, 1:-1]


def grad_x(padded):
    return padded[..., 2:, 1:-1] - padded[..., :-2, 1:-1]


def grad_y(padded):
    return padded[..., 1:-1, 2:] - padded[..., 1:-1, :-2]


def laplace(padded):
    return (
        padded[..., 2:, 1:-1]
        + padded[..., :-2, 1:-1]
        + padded[..., 1:-1, 2:]
        + padded[..., 1:-1, :-2]
        - 4.0 * center_of(padded)
    )


def advance_dynamics(zonal_pad, merid_pad, temp_pad, surf_pad, wet_mask, land_mask, coriolis_rows):
    zonal = center_of(zonal_pad)
    merid = center_of(merid_pad)
    temper = center_of(temp_pad)
    surface = center_of(surf_pad)
    divergence = jnp.sum(grad_x(zonal_pad) + grad_y(merid_pad), axis=0)
    zonal_new = wet_mask * (zonal + coriolis_rows * merid - 0.5 * grad_x(surf_pad))
    merid_new = wet_mask * (merid - coriolis_rows * zonal - 0.5 * grad_y(surf_pad))
    surface_new = land_mask * (surface - 0.25 / zonal.shape[0] * divergence)
    temper_new = wet_mask * (
        temper
        - 0.25 * (zonal * grad_x(temp_pad) + merid * grad_y(temp_pad))
        + 0.1 * laplace(temp_pad)
    )
    return (zonal_new, merid_new, temper_new, surface_new)


def advect_tracers(tracer_pad, zonal, merid, wet_mask):
    return wet_mask * (
        center_of(tracer_pad)
        - 0.25 * (zonal * grad_x(tracer_pad) + merid * grad_y(tracer_pad))
        + 0.1 * laplace(tracer_pad)
    )


def section_rows(padded, wet_mask, land_mask, coriolis_rows):
    levels = (padded.shape[0] - 1) // 3
    results = advance_dynamics(
        padded[:levels],
        padded[levels : 2 * levels],
        padded[2 * levels : 3 * levels],
        padded[3 * levels],
        wet_mask,
        land_mask,
        coriolis_rows,
    )
    return jnp.concatenate([results[0], results[1], results[2], results[3][None]], axis=0)


def body(state, depth, rates, grazing):
    groups = lax.axis_size("grp")
    member = lax.axis_index("grp")
    lat_pos = lax.axis_index("lat")
    lat_count = lax.axis_size("lat")
    local = state[0]
    field_rows, columns, lat_rows = local.shape
    total_levels = LZ * (groups - 1)
    dyn_rows = 3 * total_levels + 1
    lat_total = lat_rows * lat_count
    dyn_halo = SECTIONS + NSUB - 1
    tracer_halo = NSUB
    vel_halo = NSUB - 1

    depth_f = depth.astype(jnp.float32)
    block = jnp.concatenate([local, depth_f[None]], axis=0)
    padded = exchange(block, dyn_halo, lat_pos, lat_count)
    depth_pad = padded[field_rows]

    level_index = jnp.arange(total_levels).astype(jnp.float32)[:, None, None]
    wet_pad = (level_index < depth_pad[None]).astype(jnp.float32)
    land_pad = (depth_pad > 0).astype(jnp.float32)
    coord = (lat_pos * lat_rows - dyn_halo + jnp.arange(lat_rows + 2 * dyn_halo)).astype(jnp.float32)
    coriolis_pad = 0.3 * jnp.sin(jnp.pi * (coord + 0.5) / lat_total - jnp.pi / 2)

    def dynamics(fields, wet_pad, land_pad, coriolis_pad):
        radius = dyn_halo
        for section_index in range(SECTIONS):
            radius -= 1
            cut = dyn_halo - radius
            fields = section_rows(
                fields,
                crop(wet_pad, dyn_halo, radius),
                crop(land_pad, dyn_halo, radius),
                coriolis_pad[cut : coriolis_pad.shape[0] - cut],
            )
        return fields

    def no_dynamics(fields, wet_pad, land_pad, coriolis_pad):
        return jnp.zeros(fields.shape[:1] + crop(fields, dyn_halo, vel_halo).shape[1:], fields.dtype)

    current = lax.cond(
        member == 0, dynamics, no_dynamics, padded[:dyn_rows], wet_pad, land_pad, coriolis_pad
    )
    radius = vel_halo
    zonal_r = current[:total_levels]
    merid_r = current[total_levels : 2 * total_levels]
    temper_r = current[2 * total_levels : 3 * total_levels]
    zonal = crop(zonal_r, radius, 0)
    merid = crop(merid_r, radius, 0)
    temper = crop(temper_r, radius, 0)
    surface = crop(current[3 * total_levels], radius, 0)

    first_level = jnp.maximum(member - 1, 0) * LZ
    vcols, vrows = zonal_r.shape[-2:]
    own = None
    for shift in range(1, groups):
        levels = slice((shift - 1) * LZ, shift * LZ)
        payload = jnp.concatenate(
            [zonal_r[levels].reshape(-1), merid_r[levels].reshape(-1), temper[levels].reshape(-1)]
        )
        arrived = lax.ppermute(payload, "grp", [(0, shift)])
        own = arrived if own is None else jnp.where(member == shift, arrived, own)
    vel_size = LZ * vcols * vrows
    own_zonal = own[:vel_size].reshape(LZ, vcols, vrows)
    own_merid = own[vel_size : 2 * vel_size].reshape(LZ, vcols, vrows)
    own_temper = own[2 * vel_size :].reshape(LZ, columns, lat_rows)

    member_levels = (first_level + jnp.arange(LZ)).astype(jnp.float32)[:, None, None]
    wet_member_pad = (member_levels < depth_pad[None]).astype(jnp.float32)
    tracers = crop(padded[:field_rows], dyn_halo, tracer_halo)
    light_factor = jnp.exp(-(member_levels + 0.5) / total_levels)

    def transport(tracers, own_zonal, own_merid, own_temper, wet_member_pad, rates, grazing):
        advected = tracers.reshape((NTR, LZ) + tracers.shape[1:])
        radius = tracer_halo
        for sub_index in range(NSUB):
            radius -= 1
            advected = advect_tracers(
                advected,
                crop(own_zonal, vel_halo, radius),
                crop(own_merid, vel_halo, radius),
                crop(wet_member_pad, dyn_halo, radius),
            )
        wet_member = crop(wet_member_pad, dyn_halo, 0)
        kinetic = grazing[:, None, None, None] * (advected[0] * advected[1])[None]
        for source in range(NTR):
            kinetic = kinetic + rates[:, source, None, None, None] * advected[source][None]
        updated = wet_member[None] * (advected + 0.2 * jnp.exp(0.05 * own_temper)[None] * kinetic)
        heating = 0.3 * wet_member * updated[0] * light_factor
        return updated, heating

    def no_transport(tracers, own_zonal, own_merid, own_temper, wet_member_pad, rates, grazing):
        return (
            jnp.zeros((NTR, LZ, columns, lat_rows), jnp.float32),
            jnp.zeros((LZ, columns, lat_rows), jnp.float32),
        )

    updated, heating = lax.cond(
        member == 0,
        no_transport,
        transport,
        tracers,
        own_zonal,
        own_merid,
        own_temper,
        wet_member_pad,
        rates,
        grazing,
    )
    returned = []
    for shift in range(1, groups):
        pairs = [(shift, 0)]
        returned.append(lax.ppermute(heating, "grp", pairs))
    returned = jnp.concatenate(returned, axis=0)
    temper_final = temper + returned
    unused = jnp.zeros((field_rows - dyn_rows, columns, lat_rows), jnp.float32)
    dyn_out = jnp.concatenate([zonal, merid, temper_final, surface[None], unused], axis=0)
    result = jnp.where(member == 0, dyn_out, updated.reshape(field_rows, columns, lat_rows))
    return result[None]


def solution(mesh):
    in_specs = (P("grp", None, "lon", "lat"), P("lon", "lat"), P(), P())
    out_specs = P("grp", None, "lon", "lat")
    return jax.shard_map(body, mesh=mesh, in_specs=in_specs, out_specs=out_specs, check_vma=False)
```

```python
import jax
import jax.numpy as jnp
from jax import lax
from jax.sharding import PartitionSpec as P

LZ = 2
NTR = 20
SECTIONS = 4
NSUB = 4


def exchange(block, width, lat_pos, lat_count):
    for axis, dim in (("lat", 2), ("lon", 1)):
        count = lax.axis_size(axis)
        forward = [(i, (i + 1) % count) for i in range(count)]
        backward = [(target, source) for source, target in forward]
        low = lax.ppermute(
            lax.slice_in_dim(block, block.shape[dim] - width, None, axis=dim), axis, forward
        )
        high = lax.ppermute(lax.slice_in_dim(block, 0, width, axis=dim), axis, backward)
        block = jnp.concatenate([low, block, high], axis=dim)
    length = block.shape[-1]
    positions = jnp.arange(length)
    lower = (positions < width) & (lat_pos == 0)
    upper = (positions >= length - width) & (lat_pos == lat_count - 1)
    return jnp.where(lower | upper, 0.0, block)


def crop(array, from_radius, to_radius):
    cut = from_radius - to_radius
    if cut == 0:
        return array
    return array[..., cut : array.shape[-2] - cut, cut : array.shape[-1] - cut]


def center_of(padded):
    return padded[..., 1:-1, 1:-1]


def grad_x(padded):
    return padded[..., 2:, 1:-1] - padded[..., :-2, 1:-1]


def grad_y(padded):
    return padded[..., 1:-1, 2:] - padded[..., 1:-1, :-2]


def laplace(padded):
    return (
        padded[..., 2:, 1:-1]
        + padded[..., :-2, 1:-1]
        + padded[..., 1:-1, 2:]
        + padded[..., 1:-1, :-2]
        - 4.0 * center_of(padded)
    )


def advance_dynamics(zonal_pad, merid_pad, temp_pad, surf_pad, wet_mask, land_mask, coriolis_rows):
    zonal = center_of(zonal_pad)
    merid = center_of(merid_pad)
    temper = center_of(temp_pad)
    surface = center_of(surf_pad)
    divergence = jnp.sum(grad_x(zonal_pad) + grad_y(merid_pad), axis=0)
    zonal_new = wet_mask * (zonal + coriolis_rows * merid - 0.5 * grad_x(surf_pad))
    merid_new = wet_mask * (merid - coriolis_rows * zonal - 0.5 * grad_y(surf_pad))
    surface_new = land_mask * (surface - 0.25 / zonal.shape[0] * divergence)
    temper_new = wet_mask * (
        temper
        - 0.25 * (zonal * grad_x(temp_pad) + merid * grad_y(temp_pad))
        + 0.1 * laplace(temp_pad)
    )
    return (zonal_new, merid_new, temper_new, surface_new)


def advect_tracers(tracer_pad, zonal, merid, wet_mask):
    return wet_mask * (
        center_of(tracer_pad)
        - 0.25 * (zonal * grad_x(tracer_pad) + merid * grad_y(tracer_pad))
        + 0.1 * laplace(tracer_pad)
    )


def section_rows(padded, wet_mask, land_mask, coriolis_rows):
    levels = (padded.shape[0] - 1) // 3
    results = advance_dynamics(
        padded[:levels],
        padded[levels : 2 * levels],
        padded[2 * levels : 3 * levels],
        padded[3 * levels],
        wet_mask,
        land_mask,
        coriolis_rows,
    )
    return jnp.concatenate([results[0], results[1], results[2], results[3][None]], axis=0)


def body(state, depth, rates, grazing):
    groups = lax.axis_size("grp")
    member = lax.axis_index("grp")
    lat_pos = lax.axis_index("lat")
    lat_count = lax.axis_size("lat")
    local = state[0]
    field_rows, columns, lat_rows = local.shape
    total_levels = LZ * (groups - 1)
    dyn_rows = 3 * total_levels + 1
    lat_total = lat_rows * lat_count
    dyn_halo = SECTIONS + NSUB - 1
    tracer_halo = NSUB
    vel_halo = NSUB - 1

    depth_f = depth.astype(jnp.float32)
    block = jnp.concatenate([local, depth_f[None]], axis=0)
    padded = exchange(block, dyn_halo, lat_pos, lat_count)
    depth_pad = padded[field_rows]

    level_index = jnp.arange(total_levels).astype(jnp.float32)[:, None, None]
    wet_pad = (level_index < depth_pad[None]).astype(jnp.float32)
    land_pad = (depth_pad > 0).astype(jnp.float32)
    coord = (lat_pos * lat_rows - dyn_halo + jnp.arange(lat_rows + 2 * dyn_halo)).astype(jnp.float32)
    coriolis_pad = 0.3 * jnp.sin(jnp.pi * (coord + 0.5) / lat_total - jnp.pi / 2)

    def dynamics(fields, wet_pad, land_pad, coriolis_pad):
        radius = dyn_halo
        for section_index in range(SECTIONS):
            radius -= 1
            cut = dyn_halo - radius
            fields = section_rows(
                fields,
                crop(wet_pad, dyn_halo, radius),
                crop(land_pad, dyn_halo, radius),
                coriolis_pad[cut : coriolis_pad.shape[0] - cut],
            )
        return fields

    def no_dynamics(fields, wet_pad, land_pad, coriolis_pad):
        return jnp.zeros(fields.shape[:1] + crop(fields, dyn_halo, vel_halo).shape[1:], fields.dtype)

    current = lax.cond(
        member == 0, dynamics, no_dynamics, padded[:dyn_rows], wet_pad, land_pad, coriolis_pad
    )
    radius = vel_halo
    zonal_r = current[:total_levels]
    merid_r = current[total_levels : 2 * total_levels]
    temper_r = current[2 * total_levels : 3 * total_levels]
    zonal = crop(zonal_r, radius, 0)
    merid = crop(merid_r, radius, 0)
    temper = crop(temper_r, radius, 0)
    surface = crop(current[3 * total_levels], radius, 0)

    first_level = jnp.maximum(member - 1, 0) * LZ
    vcols, vrows = zonal_r.shape[-2:]
    own = None
    for shift in range(1, groups):
        levels = slice((shift - 1) * LZ, shift * LZ)
        payload = jnp.concatenate(
            [zonal_r[levels].reshape(-1), merid_r[levels].reshape(-1), temper[levels].reshape(-1)]
        )
        arrived = lax.ppermute(payload, "grp", [(0, shift)])
        own = arrived if own is None else jnp.where(member == shift, arrived, own)
    vel_size = LZ * vcols * vrows
    own_zonal = own[:vel_size].reshape(LZ, vcols, vrows)
    own_merid = own[vel_size : 2 * vel_size].reshape(LZ, vcols, vrows)
    own_temper = own[2 * vel_size :].reshape(LZ, columns, lat_rows)

    member_levels = (first_level + jnp.arange(LZ)).astype(jnp.float32)[:, None, None]
    wet_member_pad = (member_levels < depth_pad[None]).astype(jnp.float32)
    tracers = crop(padded[:field_rows], dyn_halo, tracer_halo)
    light_factor = jnp.exp(-(member_levels + 0.5) / total_levels)

    def transport(tracers, own_zonal, own_merid, own_temper, wet_member_pad, rates, grazing):
        advected = tracers.reshape((NTR, LZ) + tracers.shape[1:])
        radius = tracer_halo
        for sub_index in range(NSUB):
            radius -= 1
            advected = advect_tracers(
                advected,
                crop(own_zonal, vel_halo, radius),
                crop(own_merid, vel_halo, radius),
                crop(wet_member_pad, dyn_halo, radius),
            )
        wet_member = crop(wet_member_pad, dyn_halo, 0)
        kinetic = grazing[:, None, None, None] * (advected[0] * advected[1])[None]
        for source in range(NTR):
            kinetic = kinetic + rates[:, source, None, None, None] * advected[source][None]
        updated = wet_member[None] * (advected + 0.2 * jnp.exp(0.05 * own_temper)[None] * kinetic)
        heating = 0.3 * wet_member * updated[0] * light_factor
        return updated, heating

    def no_transport(tracers, own_zonal, own_merid, own_temper, wet_member_pad, rates, grazing):
        return (
            jnp.zeros((NTR, LZ, columns, lat_rows), jnp.float32),
            jnp.zeros((LZ, columns, lat_rows), jnp.float32),
        )

    updated, heating = lax.cond(
        member == 0,
        no_transport,
        transport,
        tracers,
        own_zonal,
        own_merid,
        own_temper,
        wet_member_pad,
        rates,
        grazing,
    )
    returned = []
    for shift in range(1, groups):
        pairs = [(shift, 0)]
        returned.append(lax.ppermute(heating, "grp", pairs))
    returned = jnp.concatenate(returned, axis=0)
    temper_final = temper + returned
    unused = jnp.zeros((field_rows - dyn_rows, columns, lat_rows), jnp.float32)
    dyn_out = jnp.concatenate([zonal, merid, temper_final, surface[None], unused], axis=0)
    result = jnp.where(member == 0, dyn_out, updated.reshape(field_rows, columns, lat_rows))
    return result[None]


def solution(mesh):
    in_specs = (P("grp", None, "lon", "lat"), P("lon", "lat"), P(), P())
    out_specs = P("grp", None, "lon", "lat")
    return jax.shard_map(body, mesh=mesh, in_specs=in_specs, out_specs=out_specs, check_vma=False)
```

```python
import jax
import jax.numpy as jnp
from jax import lax
from jax.sharding import PartitionSpec as P


LZ = 2
NTR = 20
SECTIONS = 4
NSUB = 4


def exchange(block, width, lat_pos, lat_count):
    for axis, dim in (("lon", 1), ("lat", 2)):
        count = lax.axis_size(axis)
        forward = [(i, (i + 1) % count) for i in range(count)]
        backward = [(target, source) for source, target in forward]
        low = lax.ppermute(
            lax.slice_in_dim(block, block.shape[dim] - width, None, axis=dim), axis, forward
        )
        high = lax.ppermute(lax.slice_in_dim(block, 0, width, axis=dim), axis, backward)
        block = jnp.concatenate([low, block, high], axis=dim)
    length = block.shape[-1]
    positions = jnp.arange(length)
    lower = (positions < width) & (lat_pos == 0)
    upper = (positions >= length - width) & (lat_pos == lat_count - 1)
    return jnp.where(lower | upper, 0.0, block)


def crop(array, from_radius, to_radius):
    cut = from_radius - to_radius
    if cut == 0:
        return array
    return array[..., cut : array.shape[-2] - cut, cut : array.shape[-1] - cut]


def center_of(padded):
    return padded[..., 1:-1, 1:-1]


def grad_x(padded):
    return padded[..., 2:, 1:-1] - padded[..., :-2, 1:-1]


def grad_y(padded):
    return padded[..., 1:-1, 2:] - padded[..., 1:-1, :-2]


def laplace(padded):
    return (
        padded[..., 2:, 1:-1]
        + padded[..., :-2, 1:-1]
        + padded[..., 1:-1, 2:]
        + padded[..., 1:-1, :-2]
        - 4.0 * center_of(padded)
    )


def advance_dynamics(zonal_pad, merid_pad, temp_pad, surf_pad, wet_mask, land_mask, coriolis_rows):
    zonal = center_of(zonal_pad)
    merid = center_of(merid_pad)
    temper = center_of(temp_pad)
    surface = center_of(surf_pad)
    divergence = jnp.sum(grad_x(zonal_pad) + grad_y(merid_pad), axis=0)
    zonal_new = wet_mask * (zonal + coriolis_rows * merid - 0.5 * grad_x(surf_pad))
    merid_new = wet_mask * (merid - coriolis_rows * zonal - 0.5 * grad_y(surf_pad))
    surface_new = land_mask * (surface - 0.25 / zonal.shape[0] * divergence)
    temper_new = wet_mask * (
        temper
        - 0.25 * (zonal * grad_x(temp_pad) + merid * grad_y(temp_pad))
        + 0.1 * laplace(temp_pad)
    )
    return (zonal_new, merid_new, temper_new, surface_new)


def advect_tracers(tracer_pad, zonal, merid, wet_mask):
    return wet_mask * (
        center_of(tracer_pad)
        - 0.25 * (zonal * grad_x(tracer_pad) + merid * grad_y(tracer_pad))
        + 0.1 * laplace(tracer_pad)
    )


def section_rows(padded, wet_mask, land_mask, coriolis_rows):
    levels = (padded.shape[0] - 1) // 3
    results = advance_dynamics(
        padded[:levels],
        padded[levels : 2 * levels],
        padded[2 * levels : 3 * levels],
        padded[3 * levels],
        wet_mask,
        land_mask,
        coriolis_rows,
    )
    return jnp.concatenate([results[0], results[1], results[2], results[3][None]], axis=0)


def step_body(state, depth, rates, grazing):
    groups = lax.axis_size("grp")
    member = lax.axis_index("grp")
    lat_pos = lax.axis_index("lat")
    lat_count = lax.axis_size("lat")
    local = state[0]
    field_rows, columns, lat_rows = local.shape
    total_levels = LZ * (groups - 1)
    dyn_rows = 3 * total_levels + 1
    lat_total = lat_rows * lat_count
    dyn_halo = SECTIONS + NSUB - 1
    tracer_halo = NSUB
    vel_halo = NSUB - 1

    depth_f = depth.astype(jnp.float32)
    block = jnp.concatenate([local, depth_f[None]], axis=0)
    padded = exchange(block, dyn_halo, lat_pos, lat_count)
    depth_pad = padded[field_rows]

    level_index = jnp.arange(total_levels).astype(jnp.float32)[:, None, None]
    wet_pad = (level_index < depth_pad[None]).astype(jnp.float32)
    land_pad = (depth_pad > 0).astype(jnp.float32)
    coord = (lat_pos * lat_rows - dyn_halo + jnp.arange(lat_rows + 2 * dyn_halo)).astype(jnp.float32)
    coriolis_pad = 0.3 * jnp.sin(jnp.pi * (coord + 0.5) / lat_total - jnp.pi / 2)

    def dynamics(fields, wet_pad, land_pad, coriolis_pad):
        radius = dyn_halo
        for _ in range(SECTIONS):
            radius -= 1
            cut = dyn_halo - radius
            fields = section_rows(
                fields,
                crop(wet_pad, dyn_halo, radius),
                crop(land_pad, dyn_halo, radius),
                coriolis_pad[cut : coriolis_pad.shape[0] - cut],
            )
        return fields

    def no_dynamics(fields, wet_pad, land_pad, coriolis_pad):
        return jnp.zeros(fields.shape[:1] + crop(fields, dyn_halo, vel_halo).shape[1:], fields.dtype)

    current = lax.cond(
        member == 0, dynamics, no_dynamics, padded[:dyn_rows], wet_pad, land_pad, coriolis_pad
    )
    radius = vel_halo
    zonal_r = current[:total_levels]
    merid_r = current[total_levels : 2 * total_levels]
    temper_r = current[2 * total_levels : 3 * total_levels]
    zonal = crop(zonal_r, radius, 0)
    merid = crop(merid_r, radius, 0)
    temper = crop(temper_r, radius, 0)
    surface = crop(current[3 * total_levels], radius, 0)

    first_level = jnp.maximum(member - 1, 0) * LZ
    vcols, vrows = zonal_r.shape[-2:]
    own = None
    for shift in range(1, groups):
        levels = slice((shift - 1) * LZ, shift * LZ)
        payload = jnp.concatenate(
            [zonal_r[levels].reshape(-1), merid_r[levels].reshape(-1), temper[levels].reshape(-1)]
        )
        arrived = lax.ppermute(payload, "grp", [(0, shift)])
        own = arrived if own is None else jnp.where(member == shift, arrived, own)
    vel_size = LZ * vcols * vrows
    own_zonal = own[:vel_size].reshape(LZ, vcols, vrows)
    own_merid = own[vel_size : 2 * vel_size].reshape(LZ, vcols, vrows)
    own_temper = own[2 * vel_size :].reshape(LZ, columns, lat_rows)

    member_levels = (first_level + jnp.arange(LZ)).astype(jnp.float32)[:, None, None]
    wet_member_pad = (member_levels < depth_pad[None]).astype(jnp.float32)
    tracers = crop(padded[:field_rows], dyn_halo, tracer_halo)
    light_factor = jnp.exp(-(member_levels + 0.5) / total_levels)

    def transport(tracers, own_zonal, own_merid, own_temper, wet_member_pad, rates, grazing):
        advected = tracers.reshape((NTR, LZ) + tracers.shape[1:])
        radius = tracer_halo
        for _ in range(NSUB):
            radius -= 1
            advected = advect_tracers(
                advected,
                crop(own_zonal, vel_halo, radius),
                crop(own_merid, vel_halo, radius),
                crop(wet_member_pad, dyn_halo, radius),
            )
        wet_member = crop(wet_member_pad, dyn_halo, 0)
        kinetic = grazing[:, None, None, None] * (advected[0] * advected[1])[None]
        for source in range(NTR):
            kinetic = kinetic + rates[:, source, None, None, None] * advected[source][None]
        updated = wet_member[None] * (advected + 0.2 * jnp.exp(0.05 * own_temper)[None] * kinetic)
        heating = 0.3 * wet_member * updated[0] * light_factor
        return updated, heating

    def no_transport(tracers, own_zonal, own_merid, own_temper, wet_member_pad, rates, grazing):
        return (
            jnp.zeros((NTR, LZ, columns, lat_rows), jnp.float32),
            jnp.zeros((LZ, columns, lat_rows), jnp.float32),
        )

    updated, heating = lax.cond(
        member == 0,
        no_transport,
        transport,
        tracers,
        own_zonal,
        own_merid,
        own_temper,
        wet_member_pad,
        rates,
        grazing,
    )
    returned = []
    for shift in range(1, groups):
        pairs = [(shift, 0)]
        returned.append(lax.ppermute(heating, "grp", pairs))
    returned = jnp.concatenate(returned, axis=0)
    temper_final = temper + returned
    unused = jnp.zeros((field_rows - dyn_rows, columns, lat_rows), jnp.float32)
    dyn_out = jnp.concatenate([zonal, merid, temper_final, surface[None], unused], axis=0)
    result = jnp.where(member == 0, dyn_out, updated.reshape(field_rows, columns, lat_rows))
    return result[None]


def solution(mesh):
    in_specs = (P("grp", None, "lon", "lat"), P("lon", "lat"), P(), P())
    out_specs = P("grp", None, "lon", "lat")
    return jax.shard_map(step_body, mesh=mesh, in_specs=in_specs, out_specs=out_specs, check_vma=False)
```

```python
import jax
import jax.numpy as jnp
from jax import lax
from jax.sharding import PartitionSpec as P

LZ = 2
NTR = 20
SECTIONS = 4
NSUB = 4


def exchange(block, width, lat_pos, lat_count):
    for axis, dim in (("lon", 1), ("lat", 2)):
        count = lax.axis_size(axis)
        forward = [(i, (i + 1) % count) for i in range(count)]
        backward = [(target, source) for source, target in forward]
        low = lax.ppermute(
            lax.slice_in_dim(block, block.shape[dim] - width, None, axis=dim), axis, forward
        )
        high = lax.ppermute(lax.slice_in_dim(block, 0, width, axis=dim), axis, backward)
        block = jnp.concatenate([low, block, high], axis=dim)
    length = block.shape[-1]
    positions = jnp.arange(length)
    lower = (positions < width) & (lat_pos == 0)
    upper = (positions >= length - width) & (lat_pos == lat_count - 1)
    return jnp.where(lower | upper, 0.0, block)


def crop(array, from_radius, to_radius):
    cut = from_radius - to_radius
    if cut == 0:
        return array
    return array[..., cut : array.shape[-2] - cut, cut : array.shape[-1] - cut]


def center_of(padded):
    return padded[..., 1:-1, 1:-1]


def grad_x(padded):
    return padded[..., 2:, 1:-1] - padded[..., :-2, 1:-1]


def grad_y(padded):
    return padded[..., 1:-1, 2:] - padded[..., 1:-1, :-2]


def laplace(padded):
    return (
        padded[..., 2:, 1:-1]
        + padded[..., :-2, 1:-1]
        + padded[..., 1:-1, 2:]
        + padded[..., 1:-1, :-2]
        - 4.0 * center_of(padded)
    )


def advance_dynamics(zonal_pad, merid_pad, temp_pad, surf_pad, wet_mask, land_mask, coriolis_rows):
    zonal = center_of(zonal_pad)
    merid = center_of(merid_pad)
    temper = center_of(temp_pad)
    surface = center_of(surf_pad)
    divergence = jnp.sum(grad_x(zonal_pad) + grad_y(merid_pad), axis=0)
    zonal_new = wet_mask * (zonal + coriolis_rows * merid - 0.5 * grad_x(surf_pad))
    merid_new = wet_mask * (merid - coriolis_rows * zonal - 0.5 * grad_y(surf_pad))
    surface_new = land_mask * (surface - 0.25 / zonal.shape[0] * divergence)
    temper_new = wet_mask * (
        temper
        - 0.25 * (zonal * grad_x(temp_pad) + merid * grad_y(temp_pad))
        + 0.1 * laplace(temp_pad)
    )
    return (zonal_new, merid_new, temper_new, surface_new)


def advect_tracers(tracer_pad, zonal, merid, wet_mask):
    return wet_mask * (
        center_of(tracer_pad)
        - 0.25 * (zonal * grad_x(tracer_pad) + merid * grad_y(tracer_pad))
        + 0.1 * laplace(tracer_pad)
    )


def section_rows(padded, wet_mask, land_mask, coriolis_rows):
    levels = (padded.shape[0] - 1) // 3
    results = advance_dynamics(
        padded[:levels],
        padded[levels : 2 * levels],
        padded[2 * levels : 3 * levels],
        padded[3 * levels],
        wet_mask,
        land_mask,
        coriolis_rows,
    )
    return jnp.concatenate([results[0], results[1], results[2], results[3][None]], axis=0)


def body(state, depth, rates, grazing):
    groups = lax.axis_size("grp")
    member = lax.axis_index("grp")
    lat_pos = lax.axis_index("lat")
    lat_count = lax.axis_size("lat")
    local = state[0]
    field_rows, columns, lat_rows = local.shape
    total_levels = LZ * (groups - 1)
    dyn_rows = 3 * total_levels + 1
    lat_total = lat_rows * lat_count
    dyn_halo = SECTIONS + NSUB - 1
    tracer_halo = NSUB
    vel_halo = NSUB - 1

    depth_f = depth.astype(jnp.float32)
    block = jnp.concatenate([local, depth_f[None]], axis=0)
    padded = exchange(block, dyn_halo, lat_pos, lat_count)
    depth_pad = padded[field_rows]

    level_index = jnp.arange(total_levels).astype(jnp.float32)[:, None, None]
    wet_pad = (level_index < depth_pad[None]).astype(jnp.float32)
    land_pad = (depth_pad > 0).astype(jnp.float32)
    coord = (lat_pos * lat_rows - dyn_halo + jnp.arange(lat_rows + 2 * dyn_halo)).astype(jnp.float32)
    coriolis_pad = 0.3 * jnp.sin(jnp.pi * (coord + 0.5) / lat_total - jnp.pi / 2)

    def dynamics(fields, wet_pad, land_pad, coriolis_pad):
        radius = dyn_halo
        for section_index in range(SECTIONS):
            radius -= 1
            cut = dyn_halo - radius
            fields = section_rows(
                fields,
                crop(wet_pad, dyn_halo, radius),
                crop(land_pad, dyn_halo, radius),
                coriolis_pad[cut : coriolis_pad.shape[0] - cut],
            )
        return fields

    def no_dynamics(fields, wet_pad, land_pad, coriolis_pad):
        return jnp.zeros(fields.shape[:1] + crop(fields, dyn_halo, vel_halo).shape[1:], fields.dtype)

    current = lax.cond(
        member == 0, dynamics, no_dynamics, padded[:dyn_rows], wet_pad, land_pad, coriolis_pad
    )
    radius = vel_halo
    zonal_r = current[:total_levels]
    merid_r = current[total_levels : 2 * total_levels]
    temper_r = current[2 * total_levels : 3 * total_levels]
    zonal = crop(zonal_r, radius, 0)
    merid = crop(merid_r, radius, 0)
    temper = crop(temper_r, radius, 0)
    surface = crop(current[3 * total_levels], radius, 0)

    first_level = jnp.maximum(member - 1, 0) * LZ
    vcols, vrows = zonal_r.shape[-2:]
    own = None
    for shift in range(1, groups):
        levels = slice((shift - 1) * LZ, shift * LZ)
        payload = jnp.concatenate(
            [zonal_r[levels].reshape(-1), merid_r[levels].reshape(-1), temper[levels].reshape(-1)]
        )
        arrived = lax.ppermute(payload, "grp", [(0, shift)])
        own = arrived if own is None else jnp.where(member == shift, arrived, own)
    vel_size = LZ * vcols * vrows
    own_zonal = own[:vel_size].reshape(LZ, vcols, vrows)
    own_merid = own[vel_size : 2 * vel_size].reshape(LZ, vcols, vrows)
    own_temper = own[2 * vel_size :].reshape(LZ, columns, lat_rows)

    member_levels = (first_level + jnp.arange(LZ)).astype(jnp.float32)[:, None, None]
    wet_member_pad = (member_levels < depth_pad[None]).astype(jnp.float32)
    tracers = crop(padded[:field_rows], dyn_halo, tracer_halo)
    light_factor = jnp.exp(-(member_levels + 0.5) / total_levels)

    def transport(tracers, own_zonal, own_merid, own_temper, wet_member_pad, rates, grazing):
        advected = tracers.reshape((NTR, LZ) + tracers.shape[1:])
        radius = tracer_halo
        for sub_index in range(NSUB):
            radius -= 1
            advected = advect_tracers(
                advected,
                crop(own_zonal, vel_halo, radius),
                crop(own_merid, vel_halo, radius),
                crop(wet_member_pad, dyn_halo, radius),
            )
        wet_member = crop(wet_member_pad, dyn_halo, 0)
        kinetic = grazing[:, None, None, None] * (advected[0] * advected[1])[None]
        for source in range(NTR):
            kinetic = kinetic + rates[:, source, None, None, None] * advected[source][None]
        updated = wet_member[None] * (advected + 0.2 * jnp.exp(0.05 * own_temper)[None] * kinetic)
        heating = 0.3 * wet_member * updated[0] * light_factor
        return updated, heating

    def no_transport(tracers, own_zonal, own_merid, own_temper, wet_member_pad, rates, grazing):
        return (
            jnp.zeros((NTR, LZ, columns, lat_rows), jnp.float32),
            jnp.zeros((LZ, columns, lat_rows), jnp.float32),
        )

    updated, heating = lax.cond(
        member == 0,
        no_transport,
        transport,
        tracers,
        own_zonal,
        own_merid,
        own_temper,
        wet_member_pad,
        rates,
        grazing,
    )
    returned = []
    for shift in range(1, groups):
        pairs = [(shift, 0)]
        returned.append(lax.ppermute(heating, "grp", pairs))
    returned = jnp.concatenate(returned, axis=0)

    def dynamics_out(zonal, merid, temper, surface, returned, updated):
        unused = jnp.zeros((field_rows - dyn_rows, columns, lat_rows), jnp.float32)
        return jnp.concatenate([zonal, merid, temper + returned, surface[None], unused], axis=0)

    def tracer_out(zonal, merid, temper, surface, returned, updated):
        return updated.reshape(field_rows, columns, lat_rows)

    result = lax.cond(
        member == 0, dynamics_out, tracer_out, zonal, merid, temper, surface, returned, updated
    )
    return result[None]


def solution(mesh):
    in_specs = (P("grp", None, "lon", "lat"), P("lon", "lat"), P(), P())
    out_specs = P("grp", None, "lon", "lat")
    return jax.shard_map(body, mesh=mesh, in_specs=in_specs, out_specs=out_specs, check_vma=False)
```

```python
import jax
import jax.numpy as jnp
from jax import lax
from jax.sharding import PartitionSpec as P

LZ = 2
NTR = 20
SECTIONS = 4
NSUB = 4


def exchange(block, width, lat_pos, lat_count):
    for axis, dim in (("lon", 1), ("lat", 2)):
        count = lax.axis_size(axis)
        forward = [(i, (i + 1) % count) for i in range(count)]
        backward = [(target, source) for source, target in forward]
        low = lax.ppermute(
            lax.slice_in_dim(block, block.shape[dim] - width, None, axis=dim), axis, forward
        )
        high = lax.ppermute(lax.slice_in_dim(block, 0, width, axis=dim), axis, backward)
        block = jnp.concatenate([low, block, high], axis=dim)
    length = block.shape[-1]
    positions = jnp.arange(length)
    lower = (positions < width) & (lat_pos == 0)
    upper = (positions >= length - width) & (lat_pos == lat_count - 1)
    return jnp.where(lower | upper, 0.0, block)


def crop(array, from_radius, to_radius):
    cut = from_radius - to_radius
    if cut == 0:
        return array
    return array[..., cut : array.shape[-2] - cut, cut : array.shape[-1] - cut]


def center_of(padded):
    return padded[..., 1:-1, 1:-1]


def grad_x(padded):
    return padded[..., 2:, 1:-1] - padded[..., :-2, 1:-1]


def grad_y(padded):
    return padded[..., 1:-1, 2:] - padded[..., 1:-1, :-2]


def laplace(padded):
    return (
        padded[..., 2:, 1:-1]
        + padded[..., :-2, 1:-1]
        + padded[..., 1:-1, 2:]
        + padded[..., 1:-1, :-2]
        - 4.0 * center_of(padded)
    )


def advance_dynamics(zonal_pad, merid_pad, temp_pad, surf_pad, wet_mask, land_mask, coriolis_rows):
    zonal = center_of(zonal_pad)
    merid = center_of(merid_pad)
    temper = center_of(temp_pad)
    surface = center_of(surf_pad)
    divergence = jnp.sum(grad_x(zonal_pad) + grad_y(merid_pad), axis=0)
    zonal_new = wet_mask * (zonal + coriolis_rows * merid - 0.5 * grad_x(surf_pad))
    merid_new = wet_mask * (merid - coriolis_rows * zonal - 0.5 * grad_y(surf_pad))
    surface_new = land_mask * (surface - 0.25 / zonal.shape[0] * divergence)
    temper_new = wet_mask * (
        temper
        - 0.25 * (zonal * grad_x(temp_pad) + merid * grad_y(temp_pad))
        + 0.1 * laplace(temp_pad)
    )
    return (zonal_new, merid_new, temper_new, surface_new)


def advect_tracers(tracer_pad, zonal, merid, wet_mask):
    return wet_mask * (
        center_of(tracer_pad)
        - 0.25 * (zonal * grad_x(tracer_pad) + merid * grad_y(tracer_pad))
        + 0.1 * laplace(tracer_pad)
    )


def section_rows(padded, wet_mask, land_mask, coriolis_rows):
    levels = (padded.shape[0] - 1) // 3
    results = advance_dynamics(
        padded[:levels],
        padded[levels : 2 * levels],
        padded[2 * levels : 3 * levels],
        padded[3 * levels],
        wet_mask,
        land_mask,
        coriolis_rows,
    )
    return jnp.concatenate([results[0], results[1], results[2], results[3][None]], axis=0)


def body(state, depth, rates, grazing):
    groups = lax.axis_size("grp")
    member = lax.axis_index("grp")
    lat_pos = lax.axis_index("lat")
    lat_count = lax.axis_size("lat")
    local = state[0]
    field_rows, columns, lat_rows = local.shape
    total_levels = LZ * (groups - 1)
    dyn_rows = 3 * total_levels + 1
    lat_total = lat_rows * lat_count
    dyn_halo = SECTIONS + NSUB - 1
    tracer_halo = NSUB
    vel_halo = NSUB - 1

    depth_f = depth.astype(jnp.float32)
    block = jnp.concatenate([local, depth_f[None]], axis=0)
    padded = exchange(block, dyn_halo, lat_pos, lat_count)
    depth_pad = padded[field_rows]

    level_index = jnp.arange(total_levels).astype(jnp.float32)[:, None, None]
    wet_pad = (level_index < depth_pad[None]).astype(jnp.float32)
    land_pad = (depth_pad > 0).astype(jnp.float32)
    coord = (lat_pos * lat_rows - dyn_halo + jnp.arange(lat_rows + 2 * dyn_halo)).astype(jnp.float32)
    coriolis_pad = 0.3 * jnp.sin(jnp.pi * (coord + 0.5) / lat_total - jnp.pi / 2)

    def dynamics(fields, wet_pad, land_pad, coriolis_pad):
        radius = dyn_halo
        for section_index in range(SECTIONS):
            radius -= 1
            cut = dyn_halo - radius
            fields = section_rows(
                fields,
                crop(wet_pad, dyn_halo, radius),
                crop(land_pad, dyn_halo, radius),
                coriolis_pad[cut : coriolis_pad.shape[0] - cut],
            )
        return fields

    def no_dynamics(fields, wet_pad, land_pad, coriolis_pad):
        return jnp.zeros(fields.shape[:1] + crop(fields, dyn_halo, vel_halo).shape[1:], fields.dtype)

    current = lax.cond(
        member == 0, dynamics, no_dynamics, padded[:dyn_rows], wet_pad, land_pad, coriolis_pad
    )
    radius = vel_halo
    zonal_r = current[:total_levels]
    merid_r = current[total_levels : 2 * total_levels]
    temper_r = current[2 * total_levels : 3 * total_levels]
    zonal = crop(zonal_r, radius, 0)
    merid = crop(merid_r, radius, 0)
    temper = crop(temper_r, radius, 0)
    surface = crop(current[3 * total_levels], radius, 0)

    first_level = jnp.maximum(member - 1, 0) * LZ
    vcols, vrows = zonal_r.shape[-2:]
    own = None
    for shift in range(1, groups):
        levels = slice((shift - 1) * LZ, shift * LZ)
        payload = jnp.concatenate(
            [zonal_r[levels].reshape(-1), merid_r[levels].reshape(-1), temper[levels].reshape(-1)]
        )
        arrived = lax.ppermute(payload, "grp", [(0, shift)])
        own = arrived if own is None else own + arrived
    vel_size = LZ * vcols * vrows
    own_zonal = own[:vel_size].reshape(LZ, vcols, vrows)
    own_merid = own[vel_size : 2 * vel_size].reshape(LZ, vcols, vrows)
    own_temper = own[2 * vel_size :].reshape(LZ, columns, lat_rows)

    member_levels = (first_level + jnp.arange(LZ)).astype(jnp.float32)[:, None, None]
    wet_member_pad = (member_levels < depth_pad[None]).astype(jnp.float32)
    tracers = crop(padded[:field_rows], dyn_halo, tracer_halo)
    light_factor = jnp.exp(-(member_levels + 0.5) / total_levels)

    def transport(tracers, own_zonal, own_merid, own_temper, wet_member_pad, rates, grazing):
        advected = tracers.reshape((NTR, LZ) + tracers.shape[1:])
        radius = tracer_halo
        for sub_index in range(NSUB):
            radius -= 1
            advected = advect_tracers(
                advected,
                crop(own_zonal, vel_halo, radius),
                crop(own_merid, vel_halo, radius),
                crop(wet_member_pad, dyn_halo, radius),
            )
        wet_member = crop(wet_member_pad, dyn_halo, 0)
        kinetic = grazing[:, None, None, None] * (advected[0] * advected[1])[None]
        for source in range(NTR):
            kinetic = kinetic + rates[:, source, None, None, None] * advected[source][None]
        updated = wet_member[None] * (advected + 0.2 * jnp.exp(0.05 * own_temper)[None] * kinetic)
        heating = 0.3 * wet_member * updated[0] * light_factor
        return updated, heating

    def no_transport(tracers, own_zonal, own_merid, own_temper, wet_member_pad, rates, grazing):
        return (
            jnp.zeros((NTR, LZ, columns, lat_rows), jnp.float32),
            jnp.zeros((LZ, columns, lat_rows), jnp.float32),
        )

    updated, heating = lax.cond(
        member == 0,
        no_transport,
        transport,
        tracers,
        own_zonal,
        own_merid,
        own_temper,
        wet_member_pad,
        rates,
        grazing,
    )
    returned = []
    for shift in range(1, groups):
        pairs = [(shift, 0)]
        returned.append(lax.ppermute(heating, "grp", pairs))
    returned = jnp.concatenate(returned, axis=0)
    temper_final = temper + returned
    unused = jnp.zeros((field_rows - dyn_rows, columns, lat_rows), jnp.float32)
    dyn_out = jnp.concatenate([zonal, merid, temper_final, surface[None], unused], axis=0)
    result = jnp.where(member == 0, dyn_out, updated.reshape(field_rows, columns, lat_rows))
    return result[None]


def solution(mesh):
    in_specs = (P("grp", None, "lon", "lat"), P("lon", "lat"), P(), P())
    out_specs = P("grp", None, "lon", "lat")
    return jax.shard_map(body, mesh=mesh, in_specs=in_specs, out_specs=out_specs, check_vma=False)
```
